32 devices in a mesh: groups: 2 (over y), ctx: 4 (over z), mp: 2 (over x), sub: 2 (over core).
Axes of the slice: x: 2, y: 2, z: 4, core: 2. Of those that a mesh axis runs over, the one named last changes fastest.
Arguments:
- features: bfloat16 [16384, 3, 4096], P(('groups', 'ctx'), None, ('mp', 'sub')), parts along dimension 0, may hold values from -6 to 6
- short_filter: float32 [7, 3, 4096], P(None, None, ('mp', 'sub')), may hold values from -2 to 2
- mr_filter: bfloat16 [256, 128], P(('mp', 'sub')), may hold values from -0.5 to 0.5
- lr_gates: bfloat16 [16384, 2, 4096], P(('groups', 'ctx'), None, ('mp', 'sub')), parts along dimension 0, may hold values from -6 to 6
- lr_rate: float32 [4096, 16], P(('mp', 'sub')), may hold values from 6.1035156e-05 to 0.05
- lr_residue: float32 [4096, 16], P(('mp', 'sub')), may hold values from -2 to 2
- lr_skip: float32 [4096], P(('mp', 'sub')), may hold values from -3 to 3
Outputs:
- output: bfloat16 [16384, 4096], P(('groups', 'ctx'), ('mp', 'sub')), parts along dimension 0
The draws below stay inside these ranges and needn't reach their ends.
There are 2 independent parts, one for each index of `groups`. The reference program is written for one: setup_inputs(seed, part) draws one part's arguments, and reference() takes and returns one part's arrays. A program takes and returns all parts, laid end to end along the dimension named above; an argument that names none is the same for every part. Nothing has to cross between parts.
All inputs are finite; a program needn't handle non-finite values.
Results may differ from the reference program's by a relative error of at most 0.0059.
Values may be sent and summed in bfloat16 or wider, within the bound.
No kernel may reach another device: no remote copies, remote signals or barrier semaphores. Data moves between devices by JAX's collectives and lax.ppermute only.
A program may use at most 192 MiB of HBM per device.

```python
import math
import jax
import jax.numpy as jnp
from jax import lax

CH = 4096
GROUP = 16
TAPS = 128
SHORT = 7
MODES = 16
SEQ = 8192


def block_levels(key, extent, cuts, smallest, high):
    gain = 1.0
    for position, parts in cuts:
        steps = jax.random.uniform(jax.random.fold_in(jax.random.fold_in(key, 6), position), (parts,), jnp.float32, smallest / len(cuts), high / len(cuts))
        gain = gain * jnp.repeat(jnp.exp(steps), extent[position] // parts).reshape((-1,) + (1,) * (len(extent) - 1 - position))
    return gain


def scatter_about(rng, extent, deviation, limit, cuts=(), held_as=jnp.bfloat16):
    result = jax.random.normal(rng, extent, jnp.float32) * deviation
    if len(cuts) > 0:
        result = block_levels(rng, extent, cuts, -0.22, 0.18) * result
    return jnp.clip(result, min=-limit, max=limit).astype(held_as)


def setup_inputs(seed: int = 0, part: int = 0) -> dict:
    seeds = jax.random.split(jax.random.key(seed), 8)
    part_keys = jax.random.split(jax.random.fold_in(seeds[7], part), 8)
    features = scatter_about(part_keys[0], (SEQ, 3, CH), 1.0, 6.0, ((0, 4), (2, 4)))
    short_filter = scatter_about(seeds[1], (SHORT, 3, CH), SHORT ** -0.5, 2.0, ((2, 4),), jnp.float32)
    mr_filter = scatter_about(seeds[2], (CH // GROUP, TAPS), TAPS ** -0.5, 0.5, ((0, 4),))
    lr_gates = scatter_about(part_keys[3], (SEQ, 2, CH), 1.0, 6.0, ((0, 4), (2, 4)))
    lr_rate = jnp.clip(jnp.exp(math.log(0.05) - 6.7083283 * jax.random.uniform(seeds[4], (CH, MODES), jnp.float32) ** block_levels(seeds[4], (CH, MODES), ((0, 4),), -0.2, 0.2)), 6.103515625e-05, 0.05)
    lr_residue = scatter_about(seeds[5], (CH, MODES), 0.35, 2.0, ((0, 4),), jnp.float32)
    lr_skip = scatter_about(seeds[6], (CH,), 0.5, 3.0, ((0, 4),), jnp.float32)
    return dict(features=features, short_filter=short_filter, mr_filter=mr_filter, lr_gates=lr_gates, lr_rate=lr_rate, lr_residue=lr_residue, lr_skip=lr_skip)


def fft_causal(signal, kernel):
    length = signal.shape[0]
    total = 2 * length
    spectrum = jnp.fft.rfft(signal, total, axis=0) * jnp.fft.rfft(kernel, total, axis=0)
    return jnp.fft.irfft(spectrum, total, axis=0)[:length]

def reference(features, short_filter, mr_filter, lr_gates, lr_rate, lr_residue, lr_skip):
    source = features.astype(jnp.float32)
    padded = jnp.pad(source, ((SHORT - 1, 0), (0, 0), (0, 0)))
    featured = jnp.zeros(source.shape, jnp.float32)
    for j in range(SHORT):
        featured = featured + short_filter[j] * padded[SHORT - 1 - j:SHORT - 1 - j + SEQ]
    query = featured[:, 0]
    product = (featured[:, 1] * featured[:, 2]).astype(jnp.bfloat16)
    blocks = CH // 256
    taps_full = jnp.repeat(mr_filter.astype(jnp.float32), GROUP, axis=0)
    signal = product.astype(jnp.float32).reshape(SEQ, blocks, 256).transpose(1, 0, 2)
    kernel = taps_full.reshape(blocks, 256, TAPS).transpose(0, 2, 1)
    mixed = lax.map(lambda pair: fft_causal(pair[0], pair[1]), (signal, kernel))
    mixed = mixed.transpose(1, 0, 2).reshape(SEQ, CH)
    lr_input = (lr_gates[:, 1] * query * mixed).astype(jnp.bfloat16)
    lr_float = lr_input.astype(jnp.float32)
    positions = jnp.arange(SEQ).astype(jnp.float32)

    def long_block(pair):
        sig, rate, resid = pair
        weight = resid * jnp.sqrt(rate)
        filt = jnp.zeros((SEQ, 256), jnp.float32)
        for r in range(MODES):
            filt = filt + weight[None, :, r] * jnp.exp(-rate[None, :, r] * positions[:, None])
        return fft_causal(sig, filt)
    signal = lr_float.reshape(SEQ, blocks, 256).transpose(1, 0, 2)
    long_mix = lax.map(long_block, (signal, lr_rate.reshape(blocks, 256, MODES), lr_residue.reshape(blocks, 256, MODES)))
    long_mix = long_mix.transpose(1, 0, 2).reshape(SEQ, CH).astype(jnp.float32)
    return (lr_gates[:, 0] * (long_mix + lr_skip * lr_float)).astype(jnp.bfloat16)
```

```python
import functools

import jax
import jax.numpy as jnp
from jax import lax
from jax.experimental import pallas as pl
from jax.experimental.pallas import tpu as pltpu
from jax.sharding import PartitionSpec as P

TAPS = 128
SHORT = 7
BLOCK = 128
LANES = 256


def passed_along(shard, axis, by):
    devices = lax.axis_size(axis)
    pairs = [(i, i + by) for i in range(devices) if 0 <= i + by < devices]
    return lax.ppermute(shard, axis, pairs)


def featurize(extended, weights):
    width = weights.shape[0]
    count = extended.shape[0] - (width - 1)
    total = jnp.zeros((count,) + extended.shape[1:], jnp.float32)
    for j in range(width):
        total = total + weights[j] * extended[width - 1 - j : width - 1 - j + count]
    return total


def medium_mix(extended, filters):
    groups, taps = filters.shape
    rows = extended.shape[0] - (taps - 1)
    chans = extended.shape[1]
    padded = jnp.concatenate([jnp.zeros((1, chans), jnp.bfloat16), extended], 0)
    blocks = rows // taps
    before = padded[:rows].reshape(blocks, taps, chans)
    current = padded[taps:].reshape(blocks, taps, chans)
    window = jnp.concatenate([before, current], 1).reshape(
        blocks, 2 * taps, groups, chans // groups
    )
    window = window.transpose(2, 3, 0, 1)
    lag = jnp.arange(taps)[:, None] + taps - jnp.arange(2 * taps)[None, :]
    pick = (lag[None] == jnp.arange(taps)[:, None, None]).astype(jnp.bfloat16)
    toeplitz = jnp.einsum("gj,jts->gts", filters, pick, preferred_element_type=jnp.float32)
    toeplitz = toeplitz.astype(jnp.bfloat16)
    mixed = jnp.einsum("gts,gkbs->gkbt", toeplitz, window, preferred_element_type=jnp.float32)
    return mixed.transpose(2, 3, 0, 1).reshape(rows, chans)


def local_kernel(x_ref, rise_ref, fall_ref, coef_ref, tri_ref, y_ref, f_ref, z_ref):
    b = pl.program_id(1)
    modes = rise_ref.shape[0]
    rows = x_ref.shape[0]

    @pl.when(b == 0)
    def _():
        z_ref[...] = jnp.zeros_like(z_ref)

    x = x_ref[...].astype(jnp.float32)
    tri = tri_ref[...]
    y = jnp.zeros(x.shape, jnp.float32)
    for r in range(modes):
        u = x * rise_ref[r]
        hi = u.astype(jnp.bfloat16)
        lo = (u - hi.astype(jnp.float32)).astype(jnp.bfloat16)
        p = jnp.dot(tri, jnp.concatenate([hi, lo], 0), preferred_element_type=jnp.float32)
        z = z_ref[r : r + 1, :]
        y = y + fall_ref[r] * (p + coef_ref[0, r : r + 1, :] * z)
        z_ref[r : r + 1, :] = coef_ref[2, r : r + 1, :] * p[rows - 1 : rows, :] + coef_ref[1, r : r + 1, :] * z
    y_ref[...] = y

    @pl.when(b == pl.num_programs(1) - 1)
    def _():
        f_ref[...] = z_ref[...]


def finish_kernel(y_ref, x_ref, gate_ref, fall_ref, coef_ref, zin_ref, skip_ref, o_ref, q_ref):
    b = pl.program_id(1)
    modes = fall_ref.shape[0]

    @pl.when(b == 0)
    def _():
        q_ref[...] = zin_ref[...] * coef_ref[0]

    corr = jnp.zeros(y_ref.shape, jnp.float32)
    for r in range(modes):
        corr = corr + fall_ref[r] * q_ref[r : r + 1, :]
    q_ref[...] = q_ref[...] * coef_ref[1]
    x = x_ref[...].astype(jnp.float32)
    total = y_ref[...] + corr + skip_ref[...] * x
    o_ref[...] = (gate_ref[...].astype(jnp.float32) * total).astype(o_ref.dtype)


def long_conv_out(lr_input, gate0, lr_rate, lr_residue, lr_skip):
    count, chans = lr_input.shape
    modes = lr_rate.shape[1]
    rows = BLOCK
    lanes = min(LANES, chans)
    blocks = count // rows
    rate = lr_rate.T
    weight = lr_residue.T * jnp.sqrt(rate)
    steps = jnp.arange(rows, dtype=jnp.float32)
    rise = jnp.exp(rate[:, None, :] * steps[None, :, None])
    fall = weight[:, None, :] * jnp.exp(-rate[:, None, :] * steps[None, :, None])
    coef = jnp.stack([jnp.exp(-rate), jnp.exp(-rate * rows), jnp.exp(-rate * (rows - 1))], 0)
    lag = jnp.arange(rows)[:, None] - jnp.arange(rows)[None, :]
    tri1 = (lag >= 0).astype(jnp.bfloat16)
    tri = jnp.concatenate([tri1, tri1], 1)
    grid = (chans // lanes, blocks)

    y, final = pl.pallas_call(
        local_kernel,
        grid=grid,
        in_specs=[
            pl.BlockSpec((rows, lanes), lambda j, b: (b, j)),
            pl.BlockSpec((modes, rows, lanes), lambda j, b: (0, 0, j)),
            pl.BlockSpec((modes, rows, lanes), lambda j, b: (0, 0, j)),
            pl.BlockSpec((3, modes, lanes), lambda j, b: (0, 0, j)),
            pl.BlockSpec((rows, 2 * rows), lambda j, b: (0, 0)),
        ],
        out_specs=[
            pl.BlockSpec((rows, lanes), lambda j, b: (b, j)),
            pl.BlockSpec((modes, lanes), lambda j, b: (0, j)),
        ],
        out_shape=[
            jax.ShapeDtypeStruct((count, chans), jnp.float32),
            jax.ShapeDtypeStruct((modes, chans), jnp.float32),
        ],
        scratch_shapes=[pltpu.VMEM((modes, lanes), jnp.float32)],
        compiler_params=pltpu.CompilerParams(dimension_semantics=("arbitrary", "arbitrary")),
    )(lr_input, rise, fall, coef, tri)

    states = lax.all_gather(final, "ctx")
    devices = states.shape[0]
    me = lax.axis_index("ctx")
    gap = (me - 1 - jnp.arange(devices)).astype(jnp.float32)
    carry = jnp.where(
        (gap >= 0)[:, None, None],
        jnp.exp(-rate[None] * (jnp.maximum(gap, 0.0) * count)[:, None, None]),
        0.0,
    )
    incoming = jnp.sum(carry * states, axis=0)

    return pl.pallas_call(
        finish_kernel,
        grid=grid,
        in_specs=[
            pl.BlockSpec((rows, lanes), lambda j, b: (b, j)),
            pl.BlockSpec((rows, lanes), lambda j, b: (b, j)),
            pl.BlockSpec((rows, lanes), lambda j, b: (b, j)),
            pl.BlockSpec((modes, rows, lanes), lambda j, b: (0, 0, j)),
            pl.BlockSpec((3, modes, lanes), lambda j, b: (0, 0, j)),
            pl.BlockSpec((modes, lanes), lambda j, b: (0, j)),
            pl.BlockSpec((1, lanes), lambda j, b: (0, j)),
        ],
        out_specs=pl.BlockSpec((rows, lanes), lambda j, b: (b, j)),
        out_shape=jax.ShapeDtypeStruct((count, chans), jnp.bfloat16),
        scratch_shapes=[pltpu.VMEM((modes, lanes), jnp.float32)],
        compiler_params=pltpu.CompilerParams(dimension_semantics=("arbitrary", "arbitrary")),
    )(y, lr_input, gate0, fall, coef, incoming, lr_skip[None, :])


HALO = 144


def front_kernel(feat_ref, halo_ref, sf_ref, toep_ref, gate_ref, o_ref, ext_ref, prod_ref):
    count = feat_ref.shape[1]
    lanes = feat_ref.shape[2]
    groups = toep_ref.shape[0]
    taps = toep_ref.shape[1]
    width = sf_ref.shape[1]
    for i in range(3):
        ext_ref[i, 0:HALO, :] = halo_ref[i].astype(jnp.float32)
        ext_ref[i, HALO : HALO + count, :] = feat_ref[i].astype(jnp.float32)
    taps_row = [[sf_ref[i, j : j + 1, :] for j in range(width)] for i in range(3)]

    def plane(i, e0):
        total = taps_row[i][0] * ext_ref[i, e0 : e0 + taps, :]
        for j in range(1, width):
            total = total + taps_row[i][j] * ext_ref[i, e0 - j : e0 - j + taps, :]
        return total

    lane_group = lax.broadcasted_iota(jnp.int32, (taps, lanes), 1) // (lanes // groups)
    for t0 in range(-taps, count, taps):
        e0 = t0 + HALO
        prod = (plane(1, e0) * plane(2, e0)).astype(jnp.bfloat16)
        prod_ref[e0 : e0 + taps, :] = prod
        if t0 < 0:
            continue
        window = prod_ref[e0 - taps : e0 + taps, :]
        mixed = None
        for g in range(groups):
            res = jnp.dot(toep_ref[g], window, preferred_element_type=jnp.float32)
            mixed = res if mixed is None else jnp.where(lane_group == g, res, mixed)
        query = plane(0, e0)
        gate = gate_ref[t0 : t0 + taps, :].astype(jnp.float32)
        o_ref[t0 : t0 + taps, :] = (gate * query * mixed).astype(o_ref.dtype)


def front(planes, halo, short_filter, mr_filter, gate1):
    _, count, chans = planes.shape
    groups, taps = mr_filter.shape
    lanes = 128
    per_tile = lanes // (chans // groups)
    lag = jnp.arange(taps)[:, None] + taps - jnp.arange(2 * taps)[None, :]
    pick = (lag[None] == jnp.arange(taps)[:, None, None]).astype(jnp.bfloat16)
    toeplitz = jnp.einsum("gj,jts->gts", mr_filter, pick, preferred_element_type=jnp.float32)
    toeplitz = toeplitz.astype(jnp.bfloat16)
    sf = short_filter.transpose(1, 0, 2)
    width = sf.shape[1]
    return pl.pallas_call(
        front_kernel,
        grid=(chans // lanes,),
        in_specs=[
            pl.BlockSpec((3, count, lanes), lambda j: (0, 0, j)),
            pl.BlockSpec((3, HALO, lanes), lambda j: (0, 0, j)),
            pl.BlockSpec((3, width, lanes), lambda j: (0, 0, j)),
            pl.BlockSpec((per_tile, taps, 2 * taps), lambda j: (j, 0, 0)),
            pl.BlockSpec((count, lanes), lambda j: (0, j)),
        ],
        out_specs=pl.BlockSpec((count, lanes), lambda j: (0, j)),
        out_shape=jax.ShapeDtypeStruct((count, chans), jnp.bfloat16),
        scratch_shapes=[
            pltpu.VMEM((3, HALO + count, lanes), jnp.float32),
            pltpu.VMEM((HALO + count, lanes), jnp.bfloat16),
        ],
        compiler_params=pltpu.CompilerParams(dimension_semantics=("arbitrary",)),
    )(planes, halo, sf, toeplitz, gate1)


def per_device(features, short_filter, mr_filter, lr_gates, lr_rate, lr_residue, lr_skip):
    count = features.shape[0]
    planes = features.transpose(1, 0, 2)
    halo = passed_along(planes[:, count - HALO :], "ctx", 1)
    gates = lr_gates.transpose(1, 0, 2)
    lr_input = front(planes, halo, short_filter, mr_filter, gates[1])
    return long_conv_out(lr_input, gates[0], lr_rate, lr_residue, lr_skip)


def solution(mesh):
    in_specs = (
        P(("groups", "ctx"), None, ("mp", "sub")),
        P(None, None, ("mp", "sub")),
        P(("mp", "sub"), None),
        P(("groups", "ctx"), None, ("mp", "sub")),
        P(("mp", "sub"), None),
        P(("mp", "sub"), None),
        P(("mp", "sub")),
    )
    out_specs = P(("groups", "ctx"), ("mp", "sub"))
    return jax.shard_map(
        per_device, mesh=mesh, in_specs=in_specs, out_specs=out_specs, check_vma=False
    )
```

```python
import functools

import jax
import jax.numpy as jnp
from jax import lax
from jax.experimental import pallas as pl
from jax.experimental.pallas import tpu as pltpu
from jax.sharding import PartitionSpec as P

TAPS = 128
SHORT = 7
BLOCK = 128
LANES = 256


def passed_along(shard, axis, by):
    devices = lax.axis_size(axis)
    pairs = [(i, i + by) for i in range(devices) if 0 <= i + by < devices]
    return lax.ppermute(shard, axis, pairs)


def featurize(extended, weights):
    width = weights.shape[0]
    count = extended.shape[0] - (width - 1)
    total = jnp.zeros((count,) + extended.shape[1:], jnp.float32)
    for j in range(width):
        total = total + weights[j] * extended[width - 1 - j : width - 1 - j + count]
    return total


def medium_mix(extended, filters):
    groups, taps = filters.shape
    rows = extended.shape[0] - (taps - 1)
    chans = extended.shape[1]
    padded = jnp.concatenate([jnp.zeros((1, chans), jnp.bfloat16), extended], 0)
    blocks = rows // taps
    before = padded[:rows].reshape(blocks, taps, chans)
    current = padded[taps:].reshape(blocks, taps, chans)
    window = jnp.concatenate([before, current], 1).reshape(
        blocks, 2 * taps, groups, chans // groups
    )
    window = window.transpose(2, 3, 0, 1)
    lag = jnp.arange(taps)[:, None] + taps - jnp.arange(2 * taps)[None, :]
    pick = (lag[None] == jnp.arange(taps)[:, None, None]).astype(jnp.bfloat16)
    toeplitz = jnp.einsum("gj,jts->gts", filters, pick, preferred_element_type=jnp.float32)
    toeplitz = toeplitz.astype(jnp.bfloat16)
    mixed = jnp.einsum("gts,gkbs->gkbt", toeplitz, window, preferred_element_type=jnp.float32)
    return mixed.transpose(2, 3, 0, 1).reshape(rows, chans)


SUB = 16
TERMS = 8


def split_pair(values):
    high = values.astype(jnp.bfloat16)
    low = (values - high.astype(jnp.float32)).astype(jnp.bfloat16)
    return high, low


def carry_subblocks(moments, z, cs_ref, l16, inter_ref=None):
    parts = []
    terms = cs_ref.shape[0]
    modes = z.shape[0]
    for sb in range(moments.shape[0] // terms):
        if inter_ref is not None:
            s = inter_ref[0] * z[0:1]
            for r in range(1, modes):
                s = s + inter_ref[r] * z[r : r + 1]
            parts.append(s)
        acc = cs_ref[0] * moments[sb * terms : sb * terms + 1]
        for n in range(1, terms):
            acc = acc + cs_ref[n] * moments[sb * terms + n : sb * terms + n + 1]
        z = l16 * z + acc
    return z, parts


def state_kernel(x_ref, mom_ref, cs_ref, l16_ref, f_ref, z_ref):
    b = pl.program_id(1)

    @pl.when(b == 0)
    def _():
        z_ref[...] = jnp.zeros_like(z_ref)

    xb = x_ref[...]
    moments = jnp.dot(mom_ref[...], jnp.concatenate([xb, xb], 0), preferred_element_type=jnp.float32)
    z, _ = carry_subblocks(moments, z_ref[...], cs_ref, l16_ref[...])
    z_ref[...] = z

    @pl.when(b == pl.num_programs(1) - 1)
    def _():
        f_ref[...] = z


def main_kernel(x_ref, gate_ref, phi_ref, mom_ref, psi_ref, ci_ref, cs_ref, inter_ref, l16_ref,
                zin_ref, skip_ref, o_ref, z_ref):
    b = pl.program_id(1)

    @pl.when(b == 0)
    def _():
        z_ref[...] = zin_ref[...]

    xb = x_ref[...]
    rows = xb.shape[0]
    x2 = jnp.concatenate([xb, xb], 0)
    near = jnp.dot(phi_ref[...], x2, preferred_element_type=jnp.float32)
    y = ci_ref[0:1] * near[0:rows]
    for n in range(1, ci_ref.shape[0]):
        y = y + ci_ref[n : n + 1] * near[n * rows : (n + 1) * rows]
    moments = jnp.dot(mom_ref[...], x2, preferred_element_type=jnp.float32)
    z, parts = carry_subblocks(moments, z_ref[...], cs_ref, l16_ref[...], inter_ref)
    z_ref[...] = z
    high, low = split_pair(jnp.concatenate(parts, 0))
    far = jnp.dot(psi_ref[...], jnp.concatenate([high, low, high], 0), preferred_element_type=jnp.float32)
    total = y + far + skip_ref[...] * xb.astype(jnp.float32)
    o_ref[...] = (gate_ref[...].astype(jnp.float32) * total).astype(o_ref.dtype)


def bases(rows):
    subs = rows // SUB
    n = jnp.arange(TERMS, dtype=jnp.float32)
    t = jnp.arange(rows)
    sb, tl = t // SUB, (t % SUB).astype(jnp.float32)
    same = sb[:, None] == sb[None, :]
    lag = (t[:, None] - t[None, :]).astype(jnp.float32)
    near = jnp.where(
        (same & (lag >= 0))[None], ((lag - 7.5) / 8.0)[None] ** n[:, None, None], 0.0
    ).reshape(TERMS * rows, rows)
    own = jnp.arange(subs)[:, None] == sb[None, :]
    mom = jnp.where(own[:, None, :], ((7.5 - tl) / 8.0)[None, None, :] ** n[None, :, None], 0.0)
    mom = mom.reshape(subs * TERMS, rows)
    psi = jnp.where(own.T[:, :, None], ((tl - 7.5) / 8.0)[:, None, None] ** n[None, None, :], 0.0)
    psi = psi.reshape(rows, subs * TERMS)
    nh, nl = split_pair(near)
    mh, ml = split_pair(mom)
    ph, pl_ = split_pair(psi)
    return (
        jnp.concatenate([nh, nl], 1),
        jnp.concatenate([mh, ml], 1),
        jnp.concatenate([ph, ph, pl_], 1),
    )


def long_conv_out(lr_input, gate0, lr_rate, lr_residue, lr_skip):
    count, chans = lr_input.shape
    modes = lr_rate.shape[1]
    rows = BLOCK
    lanes = min(LANES, chans)
    blocks = count // rows
    rate = lr_rate.T
    weight = lr_residue.T * jnp.sqrt(rate)
    n = jnp.arange(TERMS, dtype=jnp.float32)
    fact = jnp.cumprod(jnp.maximum(n, 1.0))
    powers = (-8.0 * rate)[None] ** n[:, None, None] / fact[:, None, None]
    l75 = jnp.exp(-7.5 * rate)
    cs = l75[None] * powers
    ci = jnp.sum(weight[None] * cs, axis=1)
    inter = ((weight * jnp.exp(-8.5 * rate))[None] * powers).transpose(1, 0, 2)
    l16 = jnp.exp(-float(SUB) * rate)
    phi, mom, psi = bases(rows)
    grid = (chans // lanes, blocks)
    subs_terms = mom.shape[0]
    params = pltpu.CompilerParams(dimension_semantics=("arbitrary", "arbitrary"))

    final = pl.pallas_call(
        state_kernel,
        grid=grid,
        in_specs=[
            pl.BlockSpec((rows, lanes), lambda j, b: (b, j)),
            pl.BlockSpec((subs_terms, 2 * rows), lambda j, b: (0, 0)),
            pl.BlockSpec((TERMS, modes, lanes), lambda j, b: (0, 0, j)),
            pl.BlockSpec((modes, lanes), lambda j, b: (0, j)),
        ],
        out_specs=pl.BlockSpec((modes, lanes), lambda j, b: (0, j)),
        out_shape=jax.ShapeDtypeStruct((modes, chans), jnp.float32),
        scratch_shapes=[pltpu.VMEM((modes, lanes), jnp.float32)],
        compiler_params=params,
    )(lr_input, mom, cs, l16)

    states = lax.all_gather(final, "ctx")
    devices = states.shape[0]
    me = lax.axis_index("ctx")
    gap = (me - 1 - jnp.arange(devices)).astype(jnp.float32)
    carry = jnp.where(
        (gap >= 0)[:, None, None],
        jnp.exp(-rate[None] * (jnp.maximum(gap, 0.0) * count)[:, None, None]),
        0.0,
    )
    incoming = jnp.sum(carry * states, axis=0)

    return pl.pallas_call(
        main_kernel,
        grid=grid,
        in_specs=[
            pl.BlockSpec((rows, lanes), lambda j, b: (b, j)),
            pl.BlockSpec((rows, lanes), lambda j, b: (b, j)),
            pl.BlockSpec((TERMS * rows, 2 * rows), lambda j, b: (0, 0)),
            pl.BlockSpec((subs_terms, 2 * rows), lambda j, b: (0, 0)),
            pl.BlockSpec((rows, 3 * subs_terms), lambda j, b: (0, 0)),
            pl.BlockSpec((TERMS, lanes), lambda j, b: (0, j)),
            pl.BlockSpec((TERMS, modes, lanes), lambda j, b: (0, 0, j)),
            pl.BlockSpec((modes, TERMS, lanes), lambda j, b: (0, 0, j)),
            pl.BlockSpec((modes, lanes), lambda j, b: (0, j)),
            pl.BlockSpec((modes, lanes), lambda j, b: (0, j)),
            pl.BlockSpec((1, lanes), lambda j, b: (0, j)),
        ],
        out_specs=pl.BlockSpec((rows, lanes), lambda j, b: (b, j)),
        out_shape=jax.ShapeDtypeStruct((count, chans), jnp.bfloat16),
        scratch_shapes=[pltpu.VMEM((modes, lanes), jnp.float32)],
        compiler_params=params,
    )(lr_input, gate0, phi, mom, psi, ci, cs, inter, l16, incoming, lr_skip[None, :])


HALO = 144


def front_kernel(feat_ref, halo_ref, sf_ref, toep_ref, gate_ref, o_ref, ext_ref, prod_ref):
    count = feat_ref.shape[1]
    lanes = feat_ref.shape[2]
    groups = toep_ref.shape[0]
    taps = toep_ref.shape[1]
    width = sf_ref.shape[1]
    for i in range(3):
        ext_ref[i, 0:HALO, :] = halo_ref[i].astype(jnp.float32)
        ext_ref[i, HALO : HALO + count, :] = feat_ref[i].astype(jnp.float32)
    taps_row = [[sf_ref[i, j : j + 1, :] for j in range(width)] for i in range(3)]

    def plane(i, e0):
        total = taps_row[i][0] * ext_ref[i, e0 : e0 + taps, :]
        for j in range(1, width):
            total = total + taps_row[i][j] * ext_ref[i, e0 - j : e0 - j + taps, :]
        return total

    lane_group = lax.broadcasted_iota(jnp.int32, (taps, lanes), 1) // (lanes // groups)
    for t0 in range(-taps, count, taps):
        e0 = t0 + HALO
        prod = (plane(1, e0) * plane(2, e0)).astype(jnp.bfloat16)
        prod_ref[e0 : e0 + taps, :] = prod
        if t0 < 0:
            continue
        window = prod_ref[e0 - taps : e0 + taps, :]
        mixed = None
        for g in range(groups):
            res = jnp.dot(toep_ref[g], window, preferred_element_type=jnp.float32)
            mixed = res if mixed is None else jnp.where(lane_group == g, res, mixed)
        query = plane(0, e0)
        gate = gate_ref[t0 : t0 + taps, :].astype(jnp.float32)
        o_ref[t0 : t0 + taps, :] = (gate * query * mixed).astype(o_ref.dtype)


def front(planes, halo, short_filter, mr_filter, gate1):
    _, count, chans = planes.shape
    groups, taps = mr_filter.shape
    lanes = 128
    per_tile = lanes // (chans // groups)
    lag = jnp.arange(taps)[:, None] + taps - jnp.arange(2 * taps)[None, :]
    pick = (lag[None] == jnp.arange(taps)[:, None, None]).astype(jnp.bfloat16)
    toeplitz = jnp.einsum("gj,jts->gts", mr_filter, pick, preferred_element_type=jnp.float32)
    toeplitz = toeplitz.astype(jnp.bfloat16)
    sf = short_filter.transpose(1, 0, 2)
    width = sf.shape[1]
    return pl.pallas_call(
        front_kernel,
        grid=(chans // lanes,),
        in_specs=[
            pl.BlockSpec((3, count, lanes), lambda j: (0, 0, j)),
            pl.BlockSpec((3, HALO, lanes), lambda j: (0, 0, j)),
            pl.BlockSpec((3, width, lanes), lambda j: (0, 0, j)),
            pl.BlockSpec((per_tile, taps, 2 * taps), lambda j: (j, 0, 0)),
            pl.BlockSpec((count, lanes), lambda j: (0, j)),
        ],
        out_specs=pl.BlockSpec((count, lanes), lambda j: (0, j)),
        out_shape=jax.ShapeDtypeStruct((count, chans), jnp.bfloat16),
        scratch_shapes=[
            pltpu.VMEM((3, HALO + count, lanes), jnp.float32),
            pltpu.VMEM((HALO + count, lanes), jnp.bfloat16),
        ],
        compiler_params=pltpu.CompilerParams(dimension_semantics=("arbitrary",)),
    )(planes, halo, sf, toeplitz, gate1)


def per_device(features, short_filter, mr_filter, lr_gates, lr_rate, lr_residue, lr_skip):
    count = features.shape[0]
    planes = features.transpose(1, 0, 2)
    halo = passed_along(planes[:, count - HALO :], "ctx", 1)
    gates = lr_gates.transpose(1, 0, 2)
    lr_input = front(planes, halo, short_filter, mr_filter, gates[1])
    return long_conv_out(lr_input, gates[0], lr_rate, lr_residue, lr_skip)


def solution(mesh):
    in_specs = (
        P(("groups", "ctx"), None, ("mp", "sub")),
        P(None, None, ("mp", "sub")),
        P(("mp", "sub"), None),
        P(("groups", "ctx"), None, ("mp", "sub")),
        P(("mp", "sub"), None),
        P(("mp", "sub"), None),
        P(("mp", "sub")),
    )
    out_specs = P(("groups", "ctx"), ("mp", "sub"))
    return jax.shard_map(
        per_device, mesh=mesh, in_specs=in_specs, out_specs=out_specs, check_vma=False
    )
```

```python
import functools

import jax
import jax.numpy as jnp
from jax import lax
from jax.experimental import pallas as pl
from jax.experimental.pallas import tpu as pltpu
from jax.sharding import PartitionSpec as P

TAPS = 128
SHORT = 7
BLOCK = 128
LANES = 1024


def passed_along(shard, axis, by):
    devices = lax.axis_size(axis)
    pairs = [(i, i + by) for i in range(devices) if 0 <= i + by < devices]
    return lax.ppermute(shard, axis, pairs)


def featurize(extended, weights):
    width = weights.shape[0]
    count = extended.shape[0] - (width - 1)
    total = jnp.zeros((count,) + extended.shape[1:], jnp.float32)
    for j in range(width):
        total = total + weights[j] * extended[width - 1 - j : width - 1 - j + count]
    return total


def medium_mix(extended, filters):
    groups, taps = filters.shape
    rows = extended.shape[0] - (taps - 1)
    chans = extended.shape[1]
    padded = jnp.concatenate([jnp.zeros((1, chans), jnp.bfloat16), extended], 0)
    blocks = rows // taps
    before = padded[:rows].reshape(blocks, taps, chans)
    current = padded[taps:].reshape(blocks, taps, chans)
    window = jnp.concatenate([before, current], 1).reshape(
        blocks, 2 * taps, groups, chans // groups
    )
    window = window.transpose(2, 3, 0, 1)
    lag = jnp.arange(taps)[:, None] + taps - jnp.arange(2 * taps)[None, :]
    pick = (lag[None] == jnp.arange(taps)[:, None, None]).astype(jnp.bfloat16)
    toeplitz = jnp.einsum("gj,jts->gts", filters, pick, preferred_element_type=jnp.float32)
    toeplitz = toeplitz.astype(jnp.bfloat16)
    mixed = jnp.einsum("gts,gkbs->gkbt", toeplitz, window, preferred_element_type=jnp.float32)
    return mixed.transpose(2, 3, 0, 1).reshape(rows, chans)


SUB = 16
TERMS = 8


def split_pair(values):
    high = values.astype(jnp.bfloat16)
    low = (values - high.astype(jnp.float32)).astype(jnp.bfloat16)
    return high, low


def carry_subblocks(moments, z, cs_ref, l16, inter_ref=None):
    parts = []
    terms = cs_ref.shape[0]
    modes = z.shape[0]
    for sb in range(moments.shape[0] // terms):
        if inter_ref is not None:
            s = inter_ref[0] * z[0:1]
            for r in range(1, modes):
                s = s + inter_ref[r] * z[r : r + 1]
            parts.append(s)
        acc = cs_ref[0] * moments[sb * terms : sb * terms + 1]
        for n in range(1, terms):
            acc = acc + cs_ref[n] * moments[sb * terms + n : sb * terms + n + 1]
        z = l16 * z + acc
    return z, parts


def state_kernel(x_ref, mom_ref, cs_ref, l16_ref, f_ref, z_ref):
    b = pl.program_id(1)

    @pl.when(b == 0)
    def _():
        z_ref[...] = jnp.zeros_like(z_ref)

    xb = x_ref[...]
    moments = jnp.dot(mom_ref[...], jnp.concatenate([xb, xb], 0), preferred_element_type=jnp.float32)
    z, _ = carry_subblocks(moments, z_ref[...], cs_ref, l16_ref[...])
    z_ref[...] = z

    @pl.when(b == pl.num_programs(1) - 1)
    def _():
        f_ref[...] = z


def main_kernel(x_ref, gate_ref, phi_ref, mom_ref, psi_ref, ci_ref, cs_ref, inter_ref, l16_ref,
                zin_ref, skip_ref, o_ref, z_ref):
    b = pl.program_id(1)

    @pl.when(b == 0)
    def _():
        z_ref[...] = zin_ref[...]

    xb = x_ref[...]
    rows = xb.shape[0]
    x2 = jnp.concatenate([xb, xb], 0)
    near = jnp.dot(phi_ref[...], x2, preferred_element_type=jnp.float32)
    y = ci_ref[0:1] * near[0:rows]
    for n in range(1, ci_ref.shape[0]):
        y = y + ci_ref[n : n + 1] * near[n * rows : (n + 1) * rows]
    moments = jnp.dot(mom_ref[...], x2, preferred_element_type=jnp.float32)
    z, parts = carry_subblocks(moments, z_ref[...], cs_ref, l16_ref[...], inter_ref)
    z_ref[...] = z
    high, low = split_pair(jnp.concatenate(parts, 0))
    far = jnp.dot(psi_ref[...], jnp.concatenate([high, low, high], 0), preferred_element_type=jnp.float32)
    total = y + far + skip_ref[...] * xb.astype(jnp.float32)
    o_ref[...] = (gate_ref[...].astype(jnp.float32) * total).astype(o_ref.dtype)


def bases(rows):
    subs = rows // SUB
    n = jnp.arange(TERMS, dtype=jnp.float32)
    t = jnp.arange(rows)
    sb, tl = t // SUB, (t % SUB).astype(jnp.float32)
    same = sb[:, None] == sb[None, :]
    lag = (t[:, None] - t[None, :]).astype(jnp.float32)
    near = jnp.where(
        (same & (lag >= 0))[None], ((lag - 7.5) / 8.0)[None] ** n[:, None, None], 0.0
    ).reshape(TERMS * rows, rows)
    own = jnp.arange(subs)[:, None] == sb[None, :]
    mom = jnp.where(own[:, None, :], ((7.5 - tl) / 8.0)[None, None, :] ** n[None, :, None], 0.0)
    mom = mom.reshape(subs * TERMS, rows)
    psi = jnp.where(own.T[:, :, None], ((tl - 7.5) / 8.0)[:, None, None] ** n[None, None, :], 0.0)
    psi = psi.reshape(rows, subs * TERMS)
    nh, nl = split_pair(near)
    mh, ml = split_pair(mom)
    ph, pl_ = split_pair(psi)
    return (
        jnp.concatenate([nh, nl], 1),
        jnp.concatenate([mh, ml], 1),
        jnp.concatenate([ph, ph, pl_], 1),
    )


def long_conv_out(lr_input, gate0, lr_rate, lr_residue, lr_skip):
    count, chans = lr_input.shape
    modes = lr_rate.shape[1]
    rows = BLOCK
    lanes = min(LANES, chans)
    blocks = count // rows
    rate = lr_rate.T
    weight = lr_residue.T * jnp.sqrt(rate)
    n = jnp.arange(TERMS, dtype=jnp.float32)
    fact = jnp.cumprod(jnp.maximum(n, 1.0))
    powers = (-8.0 * rate)[None] ** n[:, None, None] / fact[:, None, None]
    l75 = jnp.exp(-7.5 * rate)
    cs = l75[None] * powers
    ci = jnp.sum(weight[None] * cs, axis=1)
    inter = ((weight * jnp.exp(-8.5 * rate))[None] * powers).transpose(1, 0, 2)
    l16 = jnp.exp(-float(SUB) * rate)
    phi, mom, psi = bases(rows)
    grid = (chans // lanes, blocks)
    subs_terms = mom.shape[0]
    params = pltpu.CompilerParams(dimension_semantics=("arbitrary", "arbitrary"))

    final = pl.pallas_call(
        state_kernel,
        grid=grid,
        in_specs=[
            pl.BlockSpec((rows, lanes), lambda j, b: (b, j)),
            pl.BlockSpec((subs_terms, 2 * rows), lambda j, b: (0, 0)),
            pl.BlockSpec((TERMS, modes, lanes), lambda j, b: (0, 0, j)),
            pl.BlockSpec((modes, lanes), lambda j, b: (0, j)),
        ],
        out_specs=pl.BlockSpec((modes, lanes), lambda j, b: (0, j)),
        out_shape=jax.ShapeDtypeStruct((modes, chans), jnp.float32),
        scratch_shapes=[pltpu.VMEM((modes, lanes), jnp.float32)],
        compiler_params=params,
    )(lr_input, mom, cs, l16)

    states = lax.all_gather(final, "ctx")
    devices = states.shape[0]
    me = lax.axis_index("ctx")
    gap = (me - 1 - jnp.arange(devices)).astype(jnp.float32)
    carry = jnp.where(
        (gap >= 0)[:, None, None],
        jnp.exp(-rate[None] * (jnp.maximum(gap, 0.0) * count)[:, None, None]),
        0.0,
    )
    incoming = jnp.sum(carry * states, axis=0)

    return pl.pallas_call(
        main_kernel,
        grid=grid,
        in_specs=[
            pl.BlockSpec((rows, lanes), lambda j, b: (b, j)),
            pl.BlockSpec((rows, lanes), lambda j, b: (b, j)),
            pl.BlockSpec((TERMS * rows, 2 * rows), lambda j, b: (0, 0)),
            pl.BlockSpec((subs_terms, 2 * rows), lambda j, b: (0, 0)),
            pl.BlockSpec((rows, 3 * subs_terms), lambda j, b: (0, 0)),
            pl.BlockSpec((TERMS, lanes), lambda j, b: (0, j)),
            pl.BlockSpec((TERMS, modes, lanes), lambda j, b: (0, 0, j)),
            pl.BlockSpec((modes, TERMS, lanes), lambda j, b: (0, 0, j)),
            pl.BlockSpec((modes, lanes), lambda j, b: (0, j)),
            pl.BlockSpec((modes, lanes), lambda j, b: (0, j)),
            pl.BlockSpec((1, lanes), lambda j, b: (0, j)),
        ],
        out_specs=pl.BlockSpec((rows, lanes), lambda j, b: (b, j)),
        out_shape=jax.ShapeDtypeStruct((count, chans), jnp.bfloat16),
        scratch_shapes=[pltpu.VMEM((modes, lanes), jnp.float32)],
        compiler_params=params,
    )(lr_input, gate0, phi, mom, psi, ci, cs, inter, l16, incoming, lr_skip[None, :])


HALO = 144


def front_kernel(feat_ref, halo_ref, sf_ref, toep_ref, gate_ref, o_ref, ext_ref, prod_ref):
    count = feat_ref.shape[1]
    lanes = feat_ref.shape[2]
    groups = toep_ref.shape[0]
    taps = toep_ref.shape[1]
    width = sf_ref.shape[1]
    for i in range(3):
        ext_ref[i, 0:HALO, :] = halo_ref[i].astype(jnp.float32)
        ext_ref[i, HALO : HALO + count, :] = feat_ref[i].astype(jnp.float32)
    taps_row = [[sf_ref[i, j : j + 1, :] for j in range(width)] for i in range(3)]

    def plane(i, e0):
        total = taps_row[i][0] * ext_ref[i, e0 : e0 + taps, :]
        for j in range(1, width):
            total = total + taps_row[i][j] * ext_ref[i, e0 - j : e0 - j + taps, :]
        return total

    lane_group = lax.broadcasted_iota(jnp.int32, (taps, lanes), 1) // (lanes // groups)
    for t0 in range(-taps, count, taps):
        e0 = t0 + HALO
        prod = (plane(1, e0) * plane(2, e0)).astype(jnp.bfloat16)
        prod_ref[e0 : e0 + taps, :] = prod
        if t0 < 0:
            continue
        window = prod_ref[e0 - taps : e0 + taps, :]
        mixed = None
        for g in range(groups):
            res = jnp.dot(toep_ref[g], window, preferred_element_type=jnp.float32)
            mixed = res if mixed is None else jnp.where(lane_group == g, res, mixed)
        query = plane(0, e0)
        gate = gate_ref[t0 : t0 + taps, :].astype(jnp.float32)
        o_ref[t0 : t0 + taps, :] = (gate * query * mixed).astype(o_ref.dtype)


def front(planes, halo, short_filter, mr_filter, gate1):
    _, count, chans = planes.shape
    groups, taps = mr_filter.shape
    lanes = 128
    per_tile = lanes // (chans // groups)
    lag = jnp.arange(taps)[:, None] + taps - jnp.arange(2 * taps)[None, :]
    pick = (lag[None] == jnp.arange(taps)[:, None, None]).astype(jnp.bfloat16)
    toeplitz = jnp.einsum("gj,jts->gts", mr_filter, pick, preferred_element_type=jnp.float32)
    toeplitz = toeplitz.astype(jnp.bfloat16)
    sf = short_filter.transpose(1, 0, 2)
    width = sf.shape[1]
    return pl.pallas_call(
        front_kernel,
        grid=(chans // lanes,),
        in_specs=[
            pl.BlockSpec((3, count, lanes), lambda j: (0, 0, j)),
            pl.BlockSpec((3, HALO, lanes), lambda j: (0, 0, j)),
            pl.BlockSpec((3, width, lanes), lambda j: (0, 0, j)),
            pl.BlockSpec((per_tile, taps, 2 * taps), lambda j: (j, 0, 0)),
            pl.BlockSpec((count, lanes), lambda j: (0, j)),
        ],
        out_specs=pl.BlockSpec((count, lanes), lambda j: (0, j)),
        out_shape=jax.ShapeDtypeStruct((count, chans), jnp.bfloat16),
        scratch_shapes=[
            pltpu.VMEM((3, HALO + count, lanes), jnp.float32),
            pltpu.VMEM((HALO + count, lanes), jnp.bfloat16),
        ],
        compiler_params=pltpu.CompilerParams(dimension_semantics=("arbitrary",)),
    )(planes, halo, sf, toeplitz, gate1)


def per_device(features, short_filter, mr_filter, lr_gates, lr_rate, lr_residue, lr_skip):
    count = features.shape[0]
    planes = features.transpose(1, 0, 2)
    halo = passed_along(planes[:, count - HALO :], "ctx", 1)
    gates = lr_gates.transpose(1, 0, 2)
    lr_input = front(planes, halo, short_filter, mr_filter, gates[1])
    return long_conv_out(lr_input, gates[0], lr_rate, lr_residue, lr_skip)


def solution(mesh):
    in_specs = (
        P(("groups", "ctx"), None, ("mp", "sub")),
        P(None, None, ("mp", "sub")),
        P(("mp", "sub"), None),
        P(("groups", "ctx"), None, ("mp", "sub")),
        P(("mp", "sub"), None),
        P(("mp", "sub"), None),
        P(("mp", "sub")),
    )
    out_specs = P(("groups", "ctx"), ("mp", "sub"))
    return jax.shard_map(
        per_device, mesh=mesh, in_specs=in_specs, out_specs=out_specs, check_vma=False
    )
```

```python
import functools

import jax
import jax.numpy as jnp
from jax import lax
from jax.experimental import pallas as pl
from jax.experimental.pallas import tpu as pltpu
from jax.sharding import PartitionSpec as P

TAPS = 128
SHORT = 7
BLOCK = 128
LANES = 1024
FRONT_LANES = 512


def passed_along(shard, axis, by):
    devices = lax.axis_size(axis)
    pairs = [(i, i + by) for i in range(devices) if 0 <= i + by < devices]
    return lax.ppermute(shard, axis, pairs)


def featurize(extended, weights):
    width = weights.shape[0]
    count = extended.shape[0] - (width - 1)
    total = jnp.zeros((count,) + extended.shape[1:], jnp.float32)
    for j in range(width):
        total = total + weights[j] * extended[width - 1 - j : width - 1 - j + count]
    return total


def medium_mix(extended, filters):
    groups, taps = filters.shape
    rows = extended.shape[0] - (taps - 1)
    chans = extended.shape[1]
    padded = jnp.concatenate([jnp.zeros((1, chans), jnp.bfloat16), extended], 0)
    blocks = rows // taps
    before = padded[:rows].reshape(blocks, taps, chans)
    current = padded[taps:].reshape(blocks, taps, chans)
    window = jnp.concatenate([before, current], 1).reshape(
        blocks, 2 * taps, groups, chans // groups
    )
    window = window.transpose(2, 3, 0, 1)
    lag = jnp.arange(taps)[:, None] + taps - jnp.arange(2 * taps)[None, :]
    pick = (lag[None] == jnp.arange(taps)[:, None, None]).astype(jnp.bfloat16)
    toeplitz = jnp.einsum("gj,jts->gts", filters, pick, preferred_element_type=jnp.float32)
    toeplitz = toeplitz.astype(jnp.bfloat16)
    mixed = jnp.einsum("gts,gkbs->gkbt", toeplitz, window, preferred_element_type=jnp.float32)
    return mixed.transpose(2, 3, 0, 1).reshape(rows, chans)


SUB = 16
TERMS = 8


def split_pair(values):
    high = values.astype(jnp.bfloat16)
    low = (values - high.astype(jnp.float32)).astype(jnp.bfloat16)
    return high, low


def carry_subblocks(moments, z, cs_ref, l16, inter_ref=None):
    parts = []
    terms = cs_ref.shape[0]
    modes = z.shape[0]
    for sb in range(moments.shape[0] // terms):
        if inter_ref is not None:
            s = inter_ref[0] * z[0:1]
            for r in range(1, modes):
                s = s + inter_ref[r] * z[r : r + 1]
            parts.append(s)
        acc = cs_ref[0] * moments[sb * terms : sb * terms + 1]
        for n in range(1, terms):
            acc = acc + cs_ref[n] * moments[sb * terms + n : sb * terms + n + 1]
        z = l16 * z + acc
    return z, parts


def state_kernel(x_ref, mom_ref, cs_ref, l16_ref, f_ref, z_ref):
    b = pl.program_id(1)

    @pl.when(b == 0)
    def _():
        z_ref[...] = jnp.zeros_like(z_ref)

    xb = x_ref[...]
    moments = jnp.dot(mom_ref[...], jnp.concatenate([xb, xb], 0), preferred_element_type=jnp.float32)
    z, _ = carry_subblocks(moments, z_ref[...], cs_ref, l16_ref[...])
    z_ref[...] = z

    @pl.when(b == pl.num_programs(1) - 1)
    def _():
        f_ref[...] = z


def main_kernel(x_ref, gate_ref, phi_ref, mom_ref, psi_ref, ci_ref, cs_ref, inter_ref, l16_ref,
                zin_ref, skip_ref, o_ref, z_ref):
    b = pl.program_id(1)

    @pl.when(b == 0)
    def _():
        z_ref[...] = zin_ref[...]

    xb = x_ref[...]
    rows = xb.shape[0]
    x2 = jnp.concatenate([xb, xb], 0)
    near = jnp.dot(phi_ref[...], x2, preferred_element_type=jnp.float32)
    y = ci_ref[0:1] * near[0:rows]
    for n in range(1, ci_ref.shape[0]):
        y = y + ci_ref[n : n + 1] * near[n * rows : (n + 1) * rows]
    moments = jnp.dot(mom_ref[...], x2, preferred_element_type=jnp.float32)
    z, parts = carry_subblocks(moments, z_ref[...], cs_ref, l16_ref[...], inter_ref)
    z_ref[...] = z
    high, low = split_pair(jnp.concatenate(parts, 0))
    far = jnp.dot(psi_ref[...], jnp.concatenate([high, low, high], 0), preferred_element_type=jnp.float32)
    total = y + far + skip_ref[...] * xb.astype(jnp.float32)
    o_ref[...] = (gate_ref[...].astype(jnp.float32) * total).astype(o_ref.dtype)


def bases(rows):
    subs = rows // SUB
    n = jnp.arange(TERMS, dtype=jnp.float32)
    t = jnp.arange(rows)
    sb, tl = t // SUB, (t % SUB).astype(jnp.float32)
    same = sb[:, None] == sb[None, :]
    lag = (t[:, None] - t[None, :]).astype(jnp.float32)
    near = jnp.where(
        (same & (lag >= 0))[None], ((lag - 7.5) / 8.0)[None] ** n[:, None, None], 0.0
    ).reshape(TERMS * rows, rows)
    own = jnp.arange(subs)[:, None] == sb[None, :]
    mom = jnp.where(own[:, None, :], ((7.5 - tl) / 8.0)[None, None, :] ** n[None, :, None], 0.0)
    mom = mom.reshape(subs * TERMS, rows)
    psi = jnp.where(own.T[:, :, None], ((tl - 7.5) / 8.0)[:, None, None] ** n[None, None, :], 0.0)
    psi = psi.reshape(rows, subs * TERMS)
    nh, nl = split_pair(near)
    mh, ml = split_pair(mom)
    ph, pl_ = split_pair(psi)
    return (
        jnp.concatenate([nh, nl], 1),
        jnp.concatenate([mh, ml], 1),
        jnp.concatenate([ph, ph, pl_], 1),
    )


def long_conv_out(lr_input, gate0, lr_rate, lr_residue, lr_skip):
    count, chans = lr_input.shape
    modes = lr_rate.shape[1]
    rows = BLOCK
    lanes = min(LANES, chans)
    blocks = count // rows
    rate = lr_rate.T
    weight = lr_residue.T * jnp.sqrt(rate)
    n = jnp.arange(TERMS, dtype=jnp.float32)
    fact = jnp.cumprod(jnp.maximum(n, 1.0))
    powers = (-8.0 * rate)[None] ** n[:, None, None] / fact[:, None, None]
    l75 = jnp.exp(-7.5 * rate)
    cs = l75[None] * powers
    ci = jnp.sum(weight[None] * cs, axis=1)
    inter = ((weight * jnp.exp(-8.5 * rate))[None] * powers).transpose(1, 0, 2)
    l16 = jnp.exp(-float(SUB) * rate)
    phi, mom, psi = bases(rows)
    grid = (chans // lanes, blocks)
    subs_terms = mom.shape[0]
    params = pltpu.CompilerParams(dimension_semantics=("arbitrary", "arbitrary"))

    final = pl.pallas_call(
        state_kernel,
        grid=grid,
        in_specs=[
            pl.BlockSpec((rows, lanes), lambda j, b: (b, j)),
            pl.BlockSpec((subs_terms, 2 * rows), lambda j, b: (0, 0)),
            pl.BlockSpec((TERMS, modes, lanes), lambda j, b: (0, 0, j)),
            pl.BlockSpec((modes, lanes), lambda j, b: (0, j)),
        ],
        out_specs=pl.BlockSpec((modes, lanes), lambda j, b: (0, j)),
        out_shape=jax.ShapeDtypeStruct((modes, chans), jnp.float32),
        scratch_shapes=[pltpu.VMEM((modes, lanes), jnp.float32)],
        compiler_params=params,
    )(lr_input, mom, cs, l16)

    states = lax.all_gather(final, "ctx")
    devices = states.shape[0]
    me = lax.axis_index("ctx")
    gap = (me - 1 - jnp.arange(devices)).astype(jnp.float32)
    carry = jnp.where(
        (gap >= 0)[:, None, None],
        jnp.exp(-rate[None] * (jnp.maximum(gap, 0.0) * count)[:, None, None]),
        0.0,
    )
    incoming = jnp.sum(carry * states, axis=0)

    return pl.pallas_call(
        main_kernel,
        grid=grid,
        in_specs=[
            pl.BlockSpec((rows, lanes), lambda j, b: (b, j)),
            pl.BlockSpec((rows, lanes), lambda j, b: (b, j)),
            pl.BlockSpec((TERMS * rows, 2 * rows), lambda j, b: (0, 0)),
            pl.BlockSpec((subs_terms, 2 * rows), lambda j, b: (0, 0)),
            pl.BlockSpec((rows, 3 * subs_terms), lambda j, b: (0, 0)),
            pl.BlockSpec((TERMS, lanes), lambda j, b: (0, j)),
            pl.BlockSpec((TERMS, modes, lanes), lambda j, b: (0, 0, j)),
            pl.BlockSpec((modes, TERMS, lanes), lambda j, b: (0, 0, j)),
            pl.BlockSpec((modes, lanes), lambda j, b: (0, j)),
            pl.BlockSpec((modes, lanes), lambda j, b: (0, j)),
            pl.BlockSpec((1, lanes), lambda j, b: (0, j)),
        ],
        out_specs=pl.BlockSpec((rows, lanes), lambda j, b: (b, j)),
        out_shape=jax.ShapeDtypeStruct((count, chans), jnp.bfloat16),
        scratch_shapes=[pltpu.VMEM((modes, lanes), jnp.float32)],
        compiler_params=params,
    )(lr_input, gate0, phi, mom, psi, ci, cs, inter, l16, incoming, lr_skip[None, :])


HALO = 144


def front_kernel(feat_ref, halo_ref, sf_ref, toep_ref, gate_ref, o_ref, ext_ref, prod_ref):
    count = feat_ref.shape[1]
    lanes = feat_ref.shape[2]
    groups = toep_ref.shape[0]
    taps = toep_ref.shape[1]
    width = sf_ref.shape[1]
    for i in range(3):
        ext_ref[i, 0:HALO, :] = halo_ref[i].astype(jnp.float32)
        ext_ref[i, HALO : HALO + count, :] = feat_ref[i].astype(jnp.float32)
    taps_row = [[sf_ref[i, j : j + 1, :] for j in range(width)] for i in range(3)]

    def plane(i, e0):
        total = taps_row[i][0] * ext_ref[i, e0 : e0 + taps, :]
        for j in range(1, width):
            total = total + taps_row[i][j] * ext_ref[i, e0 - j : e0 - j + taps, :]
        return total

    chunk = 128
    per_chunk = groups * chunk // lanes
    lane_group = lax.broadcasted_iota(jnp.int32, (taps, chunk), 1) // (chunk // per_chunk)
    for t0 in range(-taps, count, taps):
        e0 = t0 + HALO
        prod = (plane(1, e0) * plane(2, e0)).astype(jnp.bfloat16)
        prod_ref[e0 : e0 + taps, :] = prod
        if t0 < 0:
            continue
        window = prod_ref[e0 - taps : e0 + taps, :]
        pieces = []
        for q in range(lanes // chunk):
            part = window[:, q * chunk : (q + 1) * chunk]
            mixed = None
            for g in range(per_chunk):
                res = jnp.dot(toep_ref[q * per_chunk + g], part, preferred_element_type=jnp.float32)
                mixed = res if mixed is None else jnp.where(lane_group == g, res, mixed)
            pieces.append(mixed)
        mixed = pieces[0] if len(pieces) == 1 else jnp.concatenate(pieces, 1)
        query = plane(0, e0)
        gate = gate_ref[t0 : t0 + taps, :].astype(jnp.float32)
        o_ref[t0 : t0 + taps, :] = (gate * query * mixed).astype(o_ref.dtype)


def front(planes, halo, short_filter, mr_filter, gate1):
    _, count, chans = planes.shape
    groups, taps = mr_filter.shape
    lanes = min(FRONT_LANES, chans)
    per_tile = lanes // (chans // groups)
    lag = jnp.arange(taps)[:, None] + taps - jnp.arange(2 * taps)[None, :]
    pick = (lag[None] == jnp.arange(taps)[:, None, None]).astype(jnp.bfloat16)
    toeplitz = jnp.einsum("gj,jts->gts", mr_filter, pick, preferred_element_type=jnp.float32)
    toeplitz = toeplitz.astype(jnp.bfloat16)
    sf = short_filter.transpose(1, 0, 2)
    width = sf.shape[1]
    return pl.pallas_call(
        front_kernel,
        grid=(chans // lanes,),
        in_specs=[
            pl.BlockSpec((3, count, lanes), lambda j: (0, 0, j)),
            pl.BlockSpec((3, HALO, lanes), lambda j: (0, 0, j)),
            pl.BlockSpec((3, width, lanes), lambda j: (0, 0, j)),
            pl.BlockSpec((per_tile, taps, 2 * taps), lambda j: (j, 0, 0)),
            pl.BlockSpec((count, lanes), lambda j: (0, j)),
        ],
        out_specs=pl.BlockSpec((count, lanes), lambda j: (0, j)),
        out_shape=jax.ShapeDtypeStruct((count, chans), jnp.bfloat16),
        scratch_shapes=[
            pltpu.VMEM((3, HALO + count, lanes), jnp.float32),
            pltpu.VMEM((HALO + count, lanes), jnp.bfloat16),
        ],
        compiler_params=pltpu.CompilerParams(dimension_semantics=("arbitrary",)),
    )(planes, halo, sf, toeplitz, gate1)


def per_device(features, short_filter, mr_filter, lr_gates, lr_rate, lr_residue, lr_skip):
    count = features.shape[0]
    planes = features.transpose(1, 0, 2)
    halo = passed_along(planes[:, count - HALO :], "ctx", 1)
    gates = lr_gates.transpose(1, 0, 2)
    lr_input = front(planes, halo, short_filter, mr_filter, gates[1])
    return long_conv_out(lr_input, gates[0], lr_rate, lr_residue, lr_skip)


def solution(mesh):
    in_specs = (
        P(("groups", "ctx"), None, ("mp", "sub")),
        P(None, None, ("mp", "sub")),
        P(("mp", "sub"), None),
        P(("groups", "ctx"), None, ("mp", "sub")),
        P(("mp", "sub"), None),
        P(("mp", "sub"), None),
        P(("mp", "sub")),
    )
    out_specs = P(("groups", "ctx"), ("mp", "sub"))
    return jax.shard_map(
        per_device, mesh=mesh, in_specs=in_specs, out_specs=out_specs, check_vma=False
    )
```

```python
import functools

import jax
import jax.numpy as jnp
from jax import lax
from jax.experimental import pallas as pl
from jax.experimental.pallas import tpu as pltpu
from jax.sharding import PartitionSpec as P

TAPS = 128
SHORT = 7
BLOCK = 128
LANES = 1024


def passed_along(shard, axis, by):
    devices = lax.axis_size(axis)
    pairs = [(i, i + by) for i in range(devices) if 0 <= i + by < devices]
    return lax.ppermute(shard, axis, pairs)


def featurize(extended, weights):
    width = weights.shape[0]
    count = extended.shape[0] - (width - 1)
    total = jnp.zeros((count,) + extended.shape[1:], jnp.float32)
    for j in range(width):
        total = total + weights[j] * extended[width - 1 - j : width - 1 - j + count]
    return total


def medium_mix(extended, filters):
    groups, taps = filters.shape
    rows = extended.shape[0] - (taps - 1)
    chans = extended.shape[1]
    padded = jnp.concatenate([jnp.zeros((1, chans), jnp.bfloat16), extended], 0)
    blocks = rows // taps
    before = padded[:rows].reshape(blocks, taps, chans)
    current = padded[taps:].reshape(blocks, taps, chans)
    window = jnp.concatenate([before, current], 1).reshape(
        blocks, 2 * taps, groups, chans // groups
    )
    window = window.transpose(2, 3, 0, 1)
    lag = jnp.arange(taps)[:, None] + taps - jnp.arange(2 * taps)[None, :]
    pick = (lag[None] == jnp.arange(taps)[:, None, None]).astype(jnp.bfloat16)
    toeplitz = jnp.einsum("gj,jts->gts", filters, pick, preferred_element_type=jnp.float32)
    toeplitz = toeplitz.astype(jnp.bfloat16)
    mixed = jnp.einsum("gts,gkbs->gkbt", toeplitz, window, preferred_element_type=jnp.float32)
    return mixed.transpose(2, 3, 0, 1).reshape(rows, chans)


SUB = 16
TERMS = 8


def split_pair(values):
    high = values.astype(jnp.bfloat16)
    low = (values - high.astype(jnp.float32)).astype(jnp.bfloat16)
    return high, low


def carry_subblocks(moments, z, cs_ref, l16, inter_ref=None):
    parts = []
    terms = cs_ref.shape[0]
    modes = z.shape[0]
    for sb in range(moments.shape[0] // terms):
        if inter_ref is not None:
            s = inter_ref[0] * z[0:1]
            for r in range(1, modes):
                s = s + inter_ref[r] * z[r : r + 1]
            parts.append(s)
        acc = cs_ref[0] * moments[sb * terms : sb * terms + 1]
        for n in range(1, terms):
            acc = acc + cs_ref[n] * moments[sb * terms + n : sb * terms + n + 1]
        z = l16 * z + acc
    return z, parts


def state_kernel(x_ref, mom_ref, cs_ref, l16_ref, f_ref, z_ref):
    b = pl.program_id(1)

    @pl.when(b == 0)
    def _():
        z_ref[...] = jnp.zeros_like(z_ref)

    xb = x_ref[...]
    moments = jnp.dot(mom_ref[...], jnp.concatenate([xb, xb], 0), preferred_element_type=jnp.float32)
    z, _ = carry_subblocks(moments, z_ref[...], cs_ref, l16_ref[...])
    z_ref[...] = z

    @pl.when(b == pl.num_programs(1) - 1)
    def _():
        f_ref[...] = z


def main_kernel(x_ref, gate_ref, phi_ref, mom_ref, psi_ref, ci_ref, cs_ref, inter_ref, l16_ref,
                zin_ref, skip_ref, o_ref, z_ref):
    b = pl.program_id(1)

    @pl.when(b == 0)
    def _():
        z_ref[...] = zin_ref[...]

    xb = x_ref[...]
    rows = xb.shape[0]
    x2 = jnp.concatenate([xb, xb], 0)
    near = jnp.dot(phi_ref[...], x2, preferred_element_type=jnp.float32)
    y = ci_ref[0:1] * near[0:rows]
    for n in range(1, ci_ref.shape[0]):
        y = y + ci_ref[n : n + 1] * near[n * rows : (n + 1) * rows]
    moments = jnp.dot(mom_ref[...], x2, preferred_element_type=jnp.float32)
    z, parts = carry_subblocks(moments, z_ref[...], cs_ref, l16_ref[...], inter_ref)
    z_ref[...] = z
    high, low = split_pair(jnp.concatenate(parts, 0))
    far = jnp.dot(psi_ref[...], jnp.concatenate([high, low, high], 0), preferred_element_type=jnp.float32)
    total = y + far + skip_ref[...] * xb.astype(jnp.float32)
    o_ref[...] = (gate_ref[:, 0, :].astype(jnp.float32) * total).astype(o_ref.dtype)


def bases(rows):
    subs = rows // SUB
    n = jnp.arange(TERMS, dtype=jnp.float32)
    t = jnp.arange(rows)
    sb, tl = t // SUB, (t % SUB).astype(jnp.float32)
    same = sb[:, None] == sb[None, :]
    lag = (t[:, None] - t[None, :]).astype(jnp.float32)
    near = jnp.where(
        (same & (lag >= 0))[None], ((lag - 7.5) / 8.0)[None] ** n[:, None, None], 0.0
    ).reshape(TERMS * rows, rows)
    own = jnp.arange(subs)[:, None] == sb[None, :]
    mom = jnp.where(own[:, None, :], ((7.5 - tl) / 8.0)[None, None, :] ** n[None, :, None], 0.0)
    mom = mom.reshape(subs * TERMS, rows)
    psi = jnp.where(own.T[:, :, None], ((tl - 7.5) / 8.0)[:, None, None] ** n[None, None, :], 0.0)
    psi = psi.reshape(rows, subs * TERMS)
    nh, nl = split_pair(near)
    mh, ml = split_pair(mom)
    ph, pl_ = split_pair(psi)
    return (
        jnp.concatenate([nh, nl], 1),
        jnp.concatenate([mh, ml], 1),
        jnp.concatenate([ph, ph, pl_], 1),
    )


def long_conv_out(lr_input, gate0, lr_rate, lr_residue, lr_skip):
    count, chans = lr_input.shape
    modes = lr_rate.shape[1]
    rows = BLOCK
    lanes = min(LANES, chans)
    blocks = count // rows
    rate = lr_rate.T
    weight = lr_residue.T * jnp.sqrt(rate)
    n = jnp.arange(TERMS, dtype=jnp.float32)
    fact = jnp.cumprod(jnp.maximum(n, 1.0))
    powers = (-8.0 * rate)[None] ** n[:, None, None] / fact[:, None, None]
    l75 = jnp.exp(-7.5 * rate)
    cs = l75[None] * powers
    ci = jnp.sum(weight[None] * cs, axis=1)
    inter = ((weight * jnp.exp(-8.5 * rate))[None] * powers).transpose(1, 0, 2)
    l16 = jnp.exp(-float(SUB) * rate)
    phi, mom, psi = bases(rows)
    grid = (chans // lanes, blocks)
    subs_terms = mom.shape[0]
    params = pltpu.CompilerParams(dimension_semantics=("arbitrary", "arbitrary"))

    final = pl.pallas_call(
        state_kernel,
        grid=grid,
        in_specs=[
            pl.BlockSpec((rows, lanes), lambda j, b: (b, j)),
            pl.BlockSpec((subs_terms, 2 * rows), lambda j, b: (0, 0)),
            pl.BlockSpec((TERMS, modes, lanes), lambda j, b: (0, 0, j)),
            pl.BlockSpec((modes, lanes), lambda j, b: (0, j)),
        ],
        out_specs=pl.BlockSpec((modes, lanes), lambda j, b: (0, j)),
        out_shape=jax.ShapeDtypeStruct((modes, chans), jnp.float32),
        scratch_shapes=[pltpu.VMEM((modes, lanes), jnp.float32)],
        compiler_params=params,
    )(lr_input, mom, cs, l16)

    states = lax.all_gather(final, "ctx")
    devices = states.shape[0]
    me = lax.axis_index("ctx")
    gap = (me - 1 - jnp.arange(devices)).astype(jnp.float32)
    carry = jnp.where(
        (gap >= 0)[:, None, None],
        jnp.exp(-rate[None] * (jnp.maximum(gap, 0.0) * count)[:, None, None]),
        0.0,
    )
    incoming = jnp.sum(carry * states, axis=0)

    return pl.pallas_call(
        main_kernel,
        grid=grid,
        in_specs=[
            pl.BlockSpec((rows, lanes), lambda j, b: (b, j)),
            pl.BlockSpec((rows, 2, lanes), lambda j, b: (b, 0, j)),
            pl.BlockSpec((TERMS * rows, 2 * rows), lambda j, b: (0, 0)),
            pl.BlockSpec((subs_terms, 2 * rows), lambda j, b: (0, 0)),
            pl.BlockSpec((rows, 3 * subs_terms), lambda j, b: (0, 0)),
            pl.BlockSpec((TERMS, lanes), lambda j, b: (0, j)),
            pl.BlockSpec((TERMS, modes, lanes), lambda j, b: (0, 0, j)),
            pl.BlockSpec((modes, TERMS, lanes), lambda j, b: (0, 0, j)),
            pl.BlockSpec((modes, lanes), lambda j, b: (0, j)),
            pl.BlockSpec((modes, lanes), lambda j, b: (0, j)),
            pl.BlockSpec((1, lanes), lambda j, b: (0, j)),
        ],
        out_specs=pl.BlockSpec((rows, lanes), lambda j, b: (b, j)),
        out_shape=jax.ShapeDtypeStruct((count, chans), jnp.bfloat16),
        scratch_shapes=[pltpu.VMEM((modes, lanes), jnp.float32)],
        compiler_params=params,
    )(lr_input, gate0, phi, mom, psi, ci, cs, inter, l16, incoming, lr_skip[None, :])


HALO = 144


def front_kernel(feat_ref, halo_ref, sf_ref, rows_ref, gate_ref, o_ref, ext_ref, prod_ref):
    count = feat_ref.shape[1]
    lanes = feat_ref.shape[2]
    groups = rows_ref.shape[0]
    taps = rows_ref.shape[1] // 2
    width = sf_ref.shape[1]
    toep = [
        pltpu.roll(
            jnp.broadcast_to(rows_ref[g : g + 1, :], (taps, 2 * taps)), 0, 1, stride=1, stride_axis=0
        ).astype(jnp.bfloat16)
        for g in range(groups)
    ]
    for i in range(3):
        ext_ref[i, 0:HALO, :] = halo_ref[i].astype(jnp.float32)
        ext_ref[i, HALO : HALO + count, :] = feat_ref[i].astype(jnp.float32)
    taps_row = [[sf_ref[i, j : j + 1, :] for j in range(width)] for i in range(3)]

    def plane(i, e0):
        total = taps_row[i][0] * ext_ref[i, e0 : e0 + taps, :]
        for j in range(1, width):
            total = total + taps_row[i][j] * ext_ref[i, e0 - j : e0 - j + taps, :]
        return total

    lane_group = lax.broadcasted_iota(jnp.int32, (taps, lanes), 1) // (lanes // groups)
    for t0 in range(-taps, count, taps):
        e0 = t0 + HALO
        prod = (plane(1, e0) * plane(2, e0)).astype(jnp.bfloat16)
        prod_ref[e0 : e0 + taps, :] = prod
        if t0 < 0:
            continue
        window = prod_ref[e0 - taps : e0 + taps, :]
        mixed = None
        for g in range(groups):
            res = jnp.dot(toep[g], window, preferred_element_type=jnp.float32)
            mixed = res if mixed is None else jnp.where(lane_group == g, res, mixed)
        query = plane(0, e0)
        gate = gate_ref[t0 : t0 + taps, 1, :].astype(jnp.float32)
        o_ref[t0 : t0 + taps, :] = (gate * query * mixed).astype(o_ref.dtype)


def front(planes, halo, short_filter, mr_filter, gates):
    _, count, chans = planes.shape
    groups, taps = mr_filter.shape
    lanes = 128
    per_tile = lanes // (chans // groups)
    template = jnp.concatenate(
        [
            jnp.zeros((groups, 1), jnp.float32),
            mr_filter[:, ::-1].astype(jnp.float32),
            jnp.zeros((groups, taps - 1), jnp.float32),
        ],
        1,
    )
    sf = short_filter.transpose(1, 0, 2)
    width = sf.shape[1]
    return pl.pallas_call(
        front_kernel,
        grid=(chans // lanes,),
        in_specs=[
            pl.BlockSpec((3, count, lanes), lambda j: (0, 0, j)),
            pl.BlockSpec((3, HALO, lanes), lambda j: (0, 0, j)),
            pl.BlockSpec((3, width, lanes), lambda j: (0, 0, j)),
            pl.BlockSpec((per_tile, 2 * taps), lambda j: (j, 0)),
            pl.BlockSpec((count, 2, lanes), lambda j: (0, 0, j)),
        ],
        out_specs=pl.BlockSpec((count, lanes), lambda j: (0, j)),
        out_shape=jax.ShapeDtypeStruct((count, chans), jnp.bfloat16),
        scratch_shapes=[
            pltpu.VMEM((3, HALO + count, lanes), jnp.float32),
            pltpu.VMEM((HALO + count, lanes), jnp.bfloat16),
        ],
        compiler_params=pltpu.CompilerParams(dimension_semantics=("arbitrary",)),
    )(planes, halo, sf, template, gates)


def per_device(features, short_filter, mr_filter, lr_gates, lr_rate, lr_residue, lr_skip):
    count = features.shape[0]
    planes = features.transpose(1, 0, 2)
    halo = passed_along(planes[:, count - HALO :], "ctx", 1)
    lr_input = front(planes, halo, short_filter, mr_filter, lr_gates)
    return long_conv_out(lr_input, lr_gates, lr_rate, lr_residue, lr_skip)


def solution(mesh):
    in_specs = (
        P(("groups", "ctx"), None, ("mp", "sub")),
        P(None, None, ("mp", "sub")),
        P(("mp", "sub"), None),
        P(("groups", "ctx"), None, ("mp", "sub")),
        P(("mp", "sub"), None),
        P(("mp", "sub"), None),
        P(("mp", "sub")),
    )
    out_specs = P(("groups", "ctx"), ("mp", "sub"))
    return jax.shard_map(
        per_device, mesh=mesh, in_specs=in_specs, out_specs=out_specs, check_vma=False
    )
```

```python
import functools

import jax
import jax.numpy as jnp
from jax import lax
from jax.experimental import pallas as pl
from jax.experimental.pallas import tpu as pltpu
from jax.sharding import PartitionSpec as P

TAPS = 128
SHORT = 7
BLOCK = 128
LANES = 1024


def passed_along(shard, axis, by):
    devices = lax.axis_size(axis)
    pairs = [(i, i + by) for i in range(devices) if 0 <= i + by < devices]
    return lax.ppermute(shard, axis, pairs)


def featurize(extended, weights):
    width = weights.shape[0]
    count = extended.shape[0] - (width - 1)
    total = jnp.zeros((count,) + extended.shape[1:], jnp.float32)
    for j in range(width):
        total = total + weights[j] * extended[width - 1 - j : width - 1 - j + count]
    return total


def medium_mix(extended, filters):
    groups, taps = filters.shape
    rows = extended.shape[0] - (taps - 1)
    chans = extended.shape[1]
    padded = jnp.concatenate([jnp.zeros((1, chans), jnp.bfloat16), extended], 0)
    blocks = rows // taps
    before = padded[:rows].reshape(blocks, taps, chans)
    current = padded[taps:].reshape(blocks, taps, chans)
    window = jnp.concatenate([before, current], 1).reshape(
        blocks, 2 * taps, groups, chans // groups
    )
    window = window.transpose(2, 3, 0, 1)
    lag = jnp.arange(taps)[:, None] + taps - jnp.arange(2 * taps)[None, :]
    pick = (lag[None] == jnp.arange(taps)[:, None, None]).astype(jnp.bfloat16)
    toeplitz = jnp.einsum("gj,jts->gts", filters, pick, preferred_element_type=jnp.float32)
    toeplitz = toeplitz.astype(jnp.bfloat16)
    mixed = jnp.einsum("gts,gkbs->gkbt", toeplitz, window, preferred_element_type=jnp.float32)
    return mixed.transpose(2, 3, 0, 1).reshape(rows, chans)


SUB = 16
TERMS = 8


def split_pair(values):
    high = values.astype(jnp.bfloat16)
    low = (values - high.astype(jnp.float32)).astype(jnp.bfloat16)
    return high, low


def carry_subblocks(moments, z, cs_ref, l16, inter_ref=None):
    parts = []
    terms = cs_ref.shape[0]
    modes = z.shape[0]
    for sb in range(moments.shape[0] // terms):
        if inter_ref is not None:
            s = inter_ref[0] * z[0:1]
            for r in range(1, modes):
                s = s + inter_ref[r] * z[r : r + 1]
            parts.append(s)
        acc = cs_ref[0] * moments[sb * terms : sb * terms + 1]
        for n in range(1, terms):
            acc = acc + cs_ref[n] * moments[sb * terms + n : sb * terms + n + 1]
        z = l16 * z + acc
    return z, parts


def state_kernel(x_ref, mom_ref, cs_ref, l16_ref, f_ref, z_ref):
    b = pl.program_id(1)

    @pl.when(b == 0)
    def _():
        z_ref[...] = jnp.zeros_like(z_ref)

    xb = x_ref[...]
    moments = jnp.dot(mom_ref[...], jnp.concatenate([xb, xb], 0), preferred_element_type=jnp.float32)
    z, _ = carry_subblocks(moments, z_ref[...], cs_ref, l16_ref[...])
    z_ref[...] = z

    @pl.when(b == pl.num_programs(1) - 1)
    def _():
        f_ref[...] = z


def main_kernel(x_ref, gate_ref, phi_ref, mom_ref, psi_ref, ci_ref, cs_ref, inter_ref, l16_ref,
                zin_ref, skip_ref, o_ref, z_ref):
    b = pl.program_id(1)

    @pl.when(b == 0)
    def _():
        z_ref[...] = zin_ref[...]

    xb = x_ref[...]
    rows = xb.shape[0]
    x2 = jnp.concatenate([xb, xb], 0)
    near = jnp.dot(phi_ref[...], x2, preferred_element_type=jnp.float32)
    y = ci_ref[0:1] * near[0:rows]
    for n in range(1, ci_ref.shape[0]):
        y = y + ci_ref[n : n + 1] * near[n * rows : (n + 1) * rows]
    moments = jnp.dot(mom_ref[...], x2, preferred_element_type=jnp.float32)
    z, parts = carry_subblocks(moments, z_ref[...], cs_ref, l16_ref[...], inter_ref)
    z_ref[...] = z
    high, low = split_pair(jnp.concatenate(parts, 0))
    far = jnp.dot(psi_ref[...], jnp.concatenate([high, low, high], 0), preferred_element_type=jnp.float32)
    total = y + far + skip_ref[...] * xb.astype(jnp.float32)
    o_ref[...] = (gate_ref[...].astype(jnp.float32) * total).astype(o_ref.dtype)


def bases(rows):
    subs = rows // SUB
    n = jnp.arange(TERMS, dtype=jnp.float32)
    t = jnp.arange(rows)
    sb, tl = t // SUB, (t % SUB).astype(jnp.float32)
    same = sb[:, None] == sb[None, :]
    lag = (t[:, None] - t[None, :]).astype(jnp.float32)
    near = jnp.where(
        (same & (lag >= 0))[None], ((lag - 7.5) / 8.0)[None] ** n[:, None, None], 0.0
    ).reshape(TERMS * rows, rows)
    own = jnp.arange(subs)[:, None] == sb[None, :]
    mom = jnp.where(own[:, None, :], ((7.5 - tl) / 8.0)[None, None, :] ** n[None, :, None], 0.0)
    mom = mom.reshape(subs * TERMS, rows)
    psi = jnp.where(own.T[:, :, None], ((tl - 7.5) / 8.0)[:, None, None] ** n[None, None, :], 0.0)
    psi = psi.reshape(rows, subs * TERMS)
    nh, nl = split_pair(near)
    mh, ml = split_pair(mom)
    ph, pl_ = split_pair(psi)
    return (
        jnp.concatenate([nh, nl], 1),
        jnp.concatenate([mh, ml], 1),
        jnp.concatenate([ph, ph, pl_], 1),
    )


def long_conv_out(lr_input, gate0, lr_rate, lr_residue, lr_skip):
    count, chans = lr_input.shape
    modes = lr_rate.shape[1]
    rows = BLOCK
    lanes = min(LANES, chans)
    blocks = count // rows
    rate = lr_rate.T
    weight = lr_residue.T * jnp.sqrt(rate)
    n = jnp.arange(TERMS, dtype=jnp.float32)
    fact = jnp.cumprod(jnp.maximum(n, 1.0))
    powers = (-8.0 * rate)[None] ** n[:, None, None] / fact[:, None, None]
    l75 = jnp.exp(-7.5 * rate)
    cs = l75[None] * powers
    ci = jnp.sum(weight[None] * cs, axis=1)
    inter = ((weight * jnp.exp(-8.5 * rate))[None] * powers).transpose(1, 0, 2)
    l16 = jnp.exp(-float(SUB) * rate)
    phi, mom, psi = bases(rows)
    grid = (chans // lanes, blocks)
    subs_terms = mom.shape[0]
    params = pltpu.CompilerParams(dimension_semantics=("arbitrary", "arbitrary"))

    final = pl.pallas_call(
        state_kernel,
        grid=grid,
        in_specs=[
            pl.BlockSpec((rows, lanes), lambda j, b: (b, j)),
            pl.BlockSpec((subs_terms, 2 * rows), lambda j, b: (0, 0)),
            pl.BlockSpec((TERMS, modes, lanes), lambda j, b: (0, 0, j)),
            pl.BlockSpec((modes, lanes), lambda j, b: (0, j)),
        ],
        out_specs=pl.BlockSpec((modes, lanes), lambda j, b: (0, j)),
        out_shape=jax.ShapeDtypeStruct((modes, chans), jnp.float32),
        scratch_shapes=[pltpu.VMEM((modes, lanes), jnp.float32)],
        compiler_params=params,
    )(lr_input, mom, cs, l16)

    states = lax.all_gather(final, "ctx")
    devices = states.shape[0]
    me = lax.axis_index("ctx")
    gap = (me - 1 - jnp.arange(devices)).astype(jnp.float32)
    carry = jnp.where(
        (gap >= 0)[:, None, None],
        jnp.exp(-rate[None] * (jnp.maximum(gap, 0.0) * count)[:, None, None]),
        0.0,
    )
    incoming = jnp.sum(carry * states, axis=0)

    return pl.pallas_call(
        main_kernel,
        grid=grid,
        in_specs=[
            pl.BlockSpec((rows, lanes), lambda j, b: (b, j)),
            pl.BlockSpec((rows, lanes), lambda j, b: (b, j)),
            pl.BlockSpec((TERMS * rows, 2 * rows), lambda j, b: (0, 0)),
            pl.BlockSpec((subs_terms, 2 * rows), lambda j, b: (0, 0)),
            pl.BlockSpec((rows, 3 * subs_terms), lambda j, b: (0, 0)),
            pl.BlockSpec((TERMS, lanes), lambda j, b: (0, j)),
            pl.BlockSpec((TERMS, modes, lanes), lambda j, b: (0, 0, j)),
            pl.BlockSpec((modes, TERMS, lanes), lambda j, b: (0, 0, j)),
            pl.BlockSpec((modes, lanes), lambda j, b: (0, j)),
            pl.BlockSpec((modes, lanes), lambda j, b: (0, j)),
            pl.BlockSpec((1, lanes), lambda j, b: (0, j)),
        ],
        out_specs=pl.BlockSpec((rows, lanes), lambda j, b: (b, j)),
        out_shape=jax.ShapeDtypeStruct((count, chans), jnp.bfloat16),
        scratch_shapes=[pltpu.VMEM((modes, lanes), jnp.float32)],
        compiler_params=params,
    )(lr_input, gate0, phi, mom, psi, ci, cs, inter, l16, incoming, lr_skip[None, :])


RIM = 8


def front_kernel(feat_ref, rim_ref, tail_ref, sf_ref, rows_ref, gate_ref, o_ref, ext_ref, prod_ref):
    count = feat_ref.shape[1]
    lanes = feat_ref.shape[2]
    groups = rows_ref.shape[0]
    taps = rows_ref.shape[1] // 2
    width = sf_ref.shape[1]
    toep = [
        pltpu.roll(
            jnp.broadcast_to(rows_ref[g : g + 1, :], (taps, 2 * taps)), 0, 1, stride=1, stride_axis=0
        ).astype(jnp.bfloat16)
        for g in range(groups)
    ]
    for i in range(3):
        ext_ref[i, 0:RIM, :] = rim_ref[i].astype(jnp.float32)
        ext_ref[i, RIM : RIM + count, :] = feat_ref[i].astype(jnp.float32)
    prod_ref[0:taps, :] = tail_ref[...]
    taps_row = [[sf_ref[i, j : j + 1, :] for j in range(width)] for i in range(3)]

    def plane(i, e0):
        total = taps_row[i][0] * ext_ref[i, e0 : e0 + taps, :]
        for j in range(1, width):
            total = total + taps_row[i][j] * ext_ref[i, e0 - j : e0 - j + taps, :]
        return total

    lane_group = lax.broadcasted_iota(jnp.int32, (taps, lanes), 1) // (lanes // groups)
    for t0 in range(0, count, taps):
        e0 = t0 + RIM
        prod = (plane(1, e0) * plane(2, e0)).astype(jnp.bfloat16)
        prod_ref[t0 + taps : t0 + 2 * taps, :] = prod
        window = prod_ref[t0 : t0 + 2 * taps, :]
        mixed = None
        for g in range(groups):
            res = jnp.dot(toep[g], window, preferred_element_type=jnp.float32)
            mixed = res if mixed is None else jnp.where(lane_group == g, res, mixed)
        query = plane(0, e0)
        gate = gate_ref[t0 : t0 + taps, :].astype(jnp.float32)
        o_ref[t0 : t0 + taps, :] = (gate * query * mixed).astype(o_ref.dtype)


def front(planes, rim, tail, short_filter, mr_filter, gate1):
    _, count, chans = planes.shape
    groups, taps = mr_filter.shape
    lanes = 128
    per_tile = lanes // (chans // groups)
    template = jnp.concatenate(
        [
            jnp.zeros((groups, 1), jnp.float32),
            mr_filter[:, ::-1].astype(jnp.float32),
            jnp.zeros((groups, taps - 1), jnp.float32),
        ],
        1,
    )
    sf = short_filter.transpose(1, 0, 2)
    width = sf.shape[1]
    return pl.pallas_call(
        front_kernel,
        grid=(chans // lanes,),
        in_specs=[
            pl.BlockSpec((3, count, lanes), lambda j: (0, 0, j)),
            pl.BlockSpec((3, RIM, lanes), lambda j: (0, 0, j)),
            pl.BlockSpec((taps, lanes), lambda j: (0, j)),
            pl.BlockSpec((3, width, lanes), lambda j: (0, 0, j)),
            pl.BlockSpec((per_tile, 2 * taps), lambda j: (j, 0)),
            pl.BlockSpec((count, lanes), lambda j: (0, j)),
        ],
        out_specs=pl.BlockSpec((count, lanes), lambda j: (0, j)),
        out_shape=jax.ShapeDtypeStruct((count, chans), jnp.bfloat16),
        scratch_shapes=[
            pltpu.VMEM((3, RIM + count, lanes), jnp.float32),
            pltpu.VMEM((taps + count, lanes), jnp.bfloat16),
        ],
        compiler_params=pltpu.CompilerParams(dimension_semantics=("arbitrary",)),
    )(planes, rim, tail, sf, template, gate1)


def per_device(features, short_filter, mr_filter, lr_gates, lr_rate, lr_residue, lr_skip):
    count = features.shape[0]
    taps = mr_filter.shape[1]
    width = short_filter.shape[0]
    planes = features.transpose(1, 0, 2)
    recent = planes[1:, count - taps - (width - 1) :].astype(jnp.float32)
    key = featurize(recent[0], short_filter[:, 1])
    value = featurize(recent[1], short_filter[:, 2])
    tail = passed_along((key * value).astype(jnp.bfloat16), "ctx", 1)
    rim = passed_along(planes[:, count - RIM :], "ctx", 1)
    lr_input = front(planes, rim, tail, short_filter, mr_filter, lr_gates[:, 1, :])
    return long_conv_out(lr_input, lr_gates[:, 0, :], lr_rate, lr_residue, lr_skip)


def solution(mesh):
    in_specs = (
        P(("groups", "ctx"), None, ("mp", "sub")),
        P(None, None, ("mp", "sub")),
        P(("mp", "sub"), None),
        P(("groups", "ctx"), None, ("mp", "sub")),
        P(("mp", "sub"), None),
        P(("mp", "sub"), None),
        P(("mp", "sub")),
    )
    out_specs = P(("groups", "ctx"), ("mp", "sub"))
    return jax.shard_map(
        per_device, mesh=mesh, in_specs=in_specs, out_specs=out_specs, check_vma=False
    )
```

```python
import functools

import jax
import jax.numpy as jnp
from jax import lax
from jax.experimental import pallas as pl
from jax.experimental.pallas import tpu as pltpu
from jax.sharding import PartitionSpec as P

TAPS = 128
SHORT = 7
BLOCK = 128
LANES = 1024


def passed_along(shard, axis, by):
    devices = lax.axis_size(axis)
    pairs = [(i, i + by) for i in range(devices) if 0 <= i + by < devices]
    return lax.ppermute(shard, axis, pairs)


def featurize(extended, weights):
    width = weights.shape[0]
    count = extended.shape[0] - (width - 1)
    total = jnp.zeros((count,) + extended.shape[1:], jnp.float32)
    for j in range(width):
        total = total + weights[j] * extended[width - 1 - j : width - 1 - j + count]
    return total


def medium_mix(extended, filters):
    groups, taps = filters.shape
    rows = extended.shape[0] - (taps - 1)
    chans = extended.shape[1]
    padded = jnp.concatenate([jnp.zeros((1, chans), jnp.bfloat16), extended], 0)
    blocks = rows // taps
    before = padded[:rows].reshape(blocks, taps, chans)
    current = padded[taps:].reshape(blocks, taps, chans)
    window = jnp.concatenate([before, current], 1).reshape(
        blocks, 2 * taps, groups, chans // groups
    )
    window = window.transpose(2, 3, 0, 1)
    lag = jnp.arange(taps)[:, None] + taps - jnp.arange(2 * taps)[None, :]
    pick = (lag[None] == jnp.arange(taps)[:, None, None]).astype(jnp.bfloat16)
    toeplitz = jnp.einsum("gj,jts->gts", filters, pick, preferred_element_type=jnp.float32)
    toeplitz = toeplitz.astype(jnp.bfloat16)
    mixed = jnp.einsum("gts,gkbs->gkbt", toeplitz, window, preferred_element_type=jnp.float32)
    return mixed.transpose(2, 3, 0, 1).reshape(rows, chans)


SUB = 16
TERMS = 8


def split_pair(values):
    high = values.astype(jnp.bfloat16)
    low = (values - high.astype(jnp.float32)).astype(jnp.bfloat16)
    return high, low


def carry_subblocks(moments, z, cs_ref, l16, inter_ref=None):
    parts = []
    terms = cs_ref.shape[0]
    modes = z.shape[0]
    for sb in range(moments.shape[0] // terms):
        if inter_ref is not None:
            s = inter_ref[0] * z[0:1]
            for r in range(1, modes):
                s = s + inter_ref[r] * z[r : r + 1]
            parts.append(s)
        acc = cs_ref[0] * moments[sb * terms : sb * terms + 1]
        for n in range(1, terms):
            acc = acc + cs_ref[n] * moments[sb * terms + n : sb * terms + n + 1]
        z = l16 * z + acc
    return z, parts


def state_kernel(x_ref, mom_ref, cs_ref, l16_ref, f_ref, z_ref):
    b = pl.program_id(1)

    @pl.when(b == 0)
    def _():
        z_ref[...] = jnp.zeros_like(z_ref)

    xb = x_ref[...]
    moments = jnp.dot(mom_ref[...], jnp.concatenate([xb, xb], 0), preferred_element_type=jnp.float32)
    z, _ = carry_subblocks(moments, z_ref[...], cs_ref, l16_ref[...])
    z_ref[...] = z

    @pl.when(b == pl.num_programs(1) - 1)
    def _():
        f_ref[...] = z


def main_kernel(x_ref, gate_ref, phi_ref, mom_ref, psi_ref, ci_ref, cs_ref, inter_ref, l16_ref,
                zin_ref, skip_ref, o_ref, z_ref):
    b = pl.program_id(1)

    @pl.when(b == 0)
    def _():
        z_ref[...] = zin_ref[...]

    xb = x_ref[...]
    rows = xb.shape[0]
    x2 = jnp.concatenate([xb, xb], 0)
    near = jnp.dot(phi_ref[...], x2, preferred_element_type=jnp.float32)
    y = ci_ref[0:1] * near[0:rows]
    for n in range(1, ci_ref.shape[0]):
        y = y + ci_ref[n : n + 1] * near[n * rows : (n + 1) * rows]
    moments = jnp.dot(mom_ref[...], x2, preferred_element_type=jnp.float32)
    z, parts = carry_subblocks(moments, z_ref[...], cs_ref, l16_ref[...], inter_ref)
    z_ref[...] = z
    high, low = split_pair(jnp.concatenate(parts, 0))
    far = jnp.dot(psi_ref[...], jnp.concatenate([high, low, high], 0), preferred_element_type=jnp.float32)
    total = y + far + skip_ref[...] * xb.astype(jnp.float32)
    o_ref[...] = (gate_ref[...].astype(jnp.float32) * total).astype(o_ref.dtype)


def bases(rows):
    subs = rows // SUB
    n = jnp.arange(TERMS, dtype=jnp.float32)
    t = jnp.arange(rows)
    sb, tl = t // SUB, (t % SUB).astype(jnp.float32)
    same = sb[:, None] == sb[None, :]
    lag = (t[:, None] - t[None, :]).astype(jnp.float32)
    near = jnp.where(
        (same & (lag >= 0))[None], ((lag - 7.5) / 8.0)[None] ** n[:, None, None], 0.0
    ).reshape(TERMS * rows, rows)
    own = jnp.arange(subs)[:, None] == sb[None, :]
    mom = jnp.where(own[:, None, :], ((7.5 - tl) / 8.0)[None, None, :] ** n[None, :, None], 0.0)
    mom = mom.reshape(subs * TERMS, rows)
    psi = jnp.where(own.T[:, :, None], ((tl - 7.5) / 8.0)[:, None, None] ** n[None, None, :], 0.0)
    psi = psi.reshape(rows, subs * TERMS)
    nh, nl = split_pair(near)
    mh, ml = split_pair(mom)
    ph, pl_ = split_pair(psi)
    return (
        jnp.concatenate([nh, nl], 1),
        jnp.concatenate([mh, ml], 1),
        jnp.concatenate([ph, ph, pl_], 1),
    )


def long_conv_out(lr_input, gate0, lr_rate, lr_residue, lr_skip):
    count, chans = lr_input.shape
    modes = lr_rate.shape[1]
    rows = BLOCK
    lanes = min(LANES, chans)
    blocks = count // rows
    rate = lr_rate.T
    weight = lr_residue.T * jnp.sqrt(rate)
    n = jnp.arange(TERMS, dtype=jnp.float32)
    fact = jnp.cumprod(jnp.maximum(n, 1.0))
    powers = (-8.0 * rate)[None] ** n[:, None, None] / fact[:, None, None]
    l75 = jnp.exp(-7.5 * rate)
    cs = l75[None] * powers
    ci = jnp.sum(weight[None] * cs, axis=1)
    inter = ((weight * jnp.exp(-8.5 * rate))[None] * powers).transpose(1, 0, 2)
    l16 = jnp.exp(-float(SUB) * rate)
    phi, mom, psi = bases(rows)
    grid = (chans // lanes, blocks)
    subs_terms = mom.shape[0]
    params = pltpu.CompilerParams(dimension_semantics=("arbitrary", "arbitrary"))

    final = pl.pallas_call(
        state_kernel,
        grid=grid,
        in_specs=[
            pl.BlockSpec((rows, lanes), lambda j, b: (b, j)),
            pl.BlockSpec((subs_terms, 2 * rows), lambda j, b: (0, 0)),
            pl.BlockSpec((TERMS, modes, lanes), lambda j, b: (0, 0, j)),
            pl.BlockSpec((modes, lanes), lambda j, b: (0, j)),
        ],
        out_specs=pl.BlockSpec((modes, lanes), lambda j, b: (0, j)),
        out_shape=jax.ShapeDtypeStruct((modes, chans), jnp.float32),
        scratch_shapes=[pltpu.VMEM((modes, lanes), jnp.float32)],
        compiler_params=params,
    )(lr_input, mom, cs, l16)

    devices = lax.axis_size("ctx")
    incoming = jnp.zeros_like(final)
    for shift in range(1, devices):
        earlier = passed_along(final, "ctx", shift)
        incoming = incoming + jnp.exp(-rate * float((shift - 1) * count)) * earlier

    return pl.pallas_call(
        main_kernel,
        grid=grid,
        in_specs=[
            pl.BlockSpec((rows, lanes), lambda j, b: (b, j)),
            pl.BlockSpec((rows, lanes), lambda j, b: (b, j)),
            pl.BlockSpec((TERMS * rows, 2 * rows), lambda j, b: (0, 0)),
            pl.BlockSpec((subs_terms, 2 * rows), lambda j, b: (0, 0)),
            pl.BlockSpec((rows, 3 * subs_terms), lambda j, b: (0, 0)),
            pl.BlockSpec((TERMS, lanes), lambda j, b: (0, j)),
            pl.BlockSpec((TERMS, modes, lanes), lambda j, b: (0, 0, j)),
            pl.BlockSpec((modes, TERMS, lanes), lambda j, b: (0, 0, j)),
            pl.BlockSpec((modes, lanes), lambda j, b: (0, j)),
            pl.BlockSpec((modes, lanes), lambda j, b: (0, j)),
            pl.BlockSpec((1, lanes), lambda j, b: (0, j)),
        ],
        out_specs=pl.BlockSpec((rows, lanes), lambda j, b: (b, j)),
        out_shape=jax.ShapeDtypeStruct((count, chans), jnp.bfloat16),
        scratch_shapes=[pltpu.VMEM((modes, lanes), jnp.float32)],
        compiler_params=params,
    )(lr_input, gate0, phi, mom, psi, ci, cs, inter, l16, incoming, lr_skip[None, :])


HALO = 144


def front_kernel(feat_ref, halo_ref, sf_ref, rows_ref, gate_ref, o_ref, ext_ref, prod_ref):
    count = feat_ref.shape[1]
    lanes = feat_ref.shape[2]
    groups = rows_ref.shape[0]
    taps = rows_ref.shape[1] // 2
    width = sf_ref.shape[1]
    toep = [
        pltpu.roll(
            jnp.broadcast_to(rows_ref[g : g + 1, :], (taps, 2 * taps)), 0, 1, stride=1, stride_axis=0
        ).astype(jnp.bfloat16)
        for g in range(groups)
    ]
    for i in range(3):
        ext_ref[i, 0:HALO, :] = halo_ref[i].astype(jnp.float32)
        ext_ref[i, HALO : HALO + count, :] = feat_ref[i].astype(jnp.float32)
    taps_row = [[sf_ref[i, j : j + 1, :] for j in range(width)] for i in range(3)]

    def plane(i, e0):
        total = taps_row[i][0] * ext_ref[i, e0 : e0 + taps, :]
        for j in range(1, width):
            total = total + taps_row[i][j] * ext_ref[i, e0 - j : e0 - j + taps, :]
        return total

    lane_group = lax.broadcasted_iota(jnp.int32, (taps, lanes), 1) // (lanes // groups)
    for t0 in range(-taps, count, taps):
        e0 = t0 + HALO
        prod = (plane(1, e0) * plane(2, e0)).astype(jnp.bfloat16)
        prod_ref[e0 : e0 + taps, :] = prod
        if t0 < 0:
            continue
        window = prod_ref[e0 - taps : e0 + taps, :]
        mixed = None
        for g in range(groups):
            res = jnp.dot(toep[g], window, preferred_element_type=jnp.float32)
            mixed = res if mixed is None else jnp.where(lane_group == g, res, mixed)
        query = plane(0, e0)
        gate = gate_ref[t0 : t0 + taps, :].astype(jnp.float32)
        o_ref[t0 : t0 + taps, :] = (gate * query * mixed).astype(o_ref.dtype)


def front(planes, halo, short_filter, mr_filter, gate1):
    _, count, chans = planes.shape
    groups, taps = mr_filter.shape
    lanes = 128
    per_tile = lanes // (chans // groups)
    template = jnp.concatenate(
        [
            jnp.zeros((groups, 1), jnp.float32),
            mr_filter[:, ::-1].astype(jnp.float32),
            jnp.zeros((groups, taps - 1), jnp.float32),
        ],
        1,
    )
    sf = short_filter.transpose(1, 0, 2)
    width = sf.shape[1]
    return pl.pallas_call(
        front_kernel,
        grid=(chans // lanes,),
        in_specs=[
            pl.BlockSpec((3, count, lanes), lambda j: (0, 0, j)),
            pl.BlockSpec((3, HALO, lanes), lambda j: (0, 0, j)),
            pl.BlockSpec((3, width, lanes), lambda j: (0, 0, j)),
            pl.BlockSpec((per_tile, 2 * taps), lambda j: (j, 0)),
            pl.BlockSpec((count, lanes), lambda j: (0, j)),
        ],
        out_specs=pl.BlockSpec((count, lanes), lambda j: (0, j)),
        out_shape=jax.ShapeDtypeStruct((count, chans), jnp.bfloat16),
        scratch_shapes=[
            pltpu.VMEM((3, HALO + count, lanes), jnp.float32),
            pltpu.VMEM((HALO + count, lanes), jnp.bfloat16),
        ],
        compiler_params=pltpu.CompilerParams(dimension_semantics=("arbitrary",)),
    )(planes, halo, sf, template, gate1)


def per_device(features, short_filter, mr_filter, lr_gates, lr_rate, lr_residue, lr_skip):
    count = features.shape[0]
    planes = features.transpose(1, 0, 2)
    halo = passed_along(planes[:, count - HALO :], "ctx", 1)
    gates = lr_gates.transpose(1, 0, 2)
    lr_input = front(planes, halo, short_filter, mr_filter, gates[1])
    return long_conv_out(lr_input, gates[0], lr_rate, lr_residue, lr_skip)


def solution(mesh):
    in_specs = (
        P(("groups", "ctx"), None, ("mp", "sub")),
        P(None, None, ("mp", "sub")),
        P(("mp", "sub"), None),
        P(("groups", "ctx"), None, ("mp", "sub")),
        P(("mp", "sub"), None),
        P(("mp", "sub"), None),
        P(("mp", "sub")),
    )
    out_specs = P(("groups", "ctx"), ("mp", "sub"))
    return jax.shard_map(
        per_device, mesh=mesh, in_specs=in_specs, out_specs=out_specs, check_vma=False
    )
```

```python
import functools

import jax
import numpy as np
import jax.numpy as jnp
from jax import lax
from jax.experimental import pallas as pl
from jax.experimental.pallas import tpu as pltpu
from jax.sharding import PartitionSpec as P

TAPS = 128
SHORT = 7
BLOCK = 128
LANES = 1024


def passed_along(shard, axis, by):
    devices = lax.axis_size(axis)
    pairs = [(i, i + by) for i in range(devices) if 0 <= i + by < devices]
    return lax.ppermute(shard, axis, pairs)


def featurize(extended, weights):
    width = weights.shape[0]
    count = extended.shape[0] - (width - 1)
    total = jnp.zeros((count,) + extended.shape[1:], jnp.float32)
    for j in range(width):
        total = total + weights[j] * extended[width - 1 - j : width - 1 - j + count]
    return total


def medium_mix(extended, filters):
    groups, taps = filters.shape
    rows = extended.shape[0] - (taps - 1)
    chans = extended.shape[1]
    padded = jnp.concatenate([jnp.zeros((1, chans), jnp.bfloat16), extended], 0)
    blocks = rows // taps
    before = padded[:rows].reshape(blocks, taps, chans)
    current = padded[taps:].reshape(blocks, taps, chans)
    window = jnp.concatenate([before, current], 1).reshape(
        blocks, 2 * taps, groups, chans // groups
    )
    window = window.transpose(2, 3, 0, 1)
    lag = jnp.arange(taps)[:, None] + taps - jnp.arange(2 * taps)[None, :]
    pick = (lag[None] == jnp.arange(taps)[:, None, None]).astype(jnp.bfloat16)
    toeplitz = jnp.einsum("gj,jts->gts", filters, pick, preferred_element_type=jnp.float32)
    toeplitz = toeplitz.astype(jnp.bfloat16)
    mixed = jnp.einsum("gts,gkbs->gkbt", toeplitz, window, preferred_element_type=jnp.float32)
    return mixed.transpose(2, 3, 0, 1).reshape(rows, chans)


SUB = 16
TERMS = 8


def split_pair(values):
    high = values.astype(jnp.bfloat16)
    low = (values - high.astype(jnp.float32)).astype(jnp.bfloat16)
    return high, low


def tree_sum(values):
    while len(values) > 1:
        values = [values[i] + values[i + 1] if i + 1 < len(values) else values[i] for i in range(0, len(values), 2)]
    return values[0]


def carry_subblocks(moments, z, cs_ref, l16, inter_ref=None):
    terms = cs_ref.shape[0]
    subs = moments.shape[0] // terms
    coefs = [cs_ref[n] for n in range(terms)]
    accs = [
        tree_sum([coefs[n] * moments[sb * terms + n : sb * terms + n + 1] for n in range(terms)])
        for sb in range(subs)
    ]
    zs = []
    for sb in range(subs):
        zs.append(z)
        z = l16 * z + accs[sb]
    parts = []
    if inter_ref is not None:
        modes = z.shape[0]
        for sb in range(subs):
            parts.append(tree_sum([inter_ref[r] * zs[sb][r : r + 1] for r in range(modes)]))
    return z, parts


def state_kernel(x_ref, mom_ref, cs_ref, l16_ref, f_ref, z_ref):
    b = pl.program_id(1)

    @pl.when(b == 0)
    def _():
        z_ref[...] = jnp.zeros_like(z_ref)

    xb = x_ref[...]
    moments = jnp.dot(mom_ref[...], jnp.concatenate([xb, xb], 0), preferred_element_type=jnp.float32)
    z, _ = carry_subblocks(moments, z_ref[...], cs_ref, l16_ref[...])
    z_ref[...] = z

    @pl.when(b == pl.num_programs(1) - 1)
    def _():
        f_ref[...] = z


def main_kernel(x_ref, gate_ref, phi_ref, mom_ref, psi_ref, ci_ref, cs_ref, inter_ref, l16_ref,
                zin_ref, skip_ref, o_ref, z_ref):
    b = pl.program_id(1)

    @pl.when(b == 0)
    def _():
        z_ref[...] = zin_ref[...]

    xb = x_ref[...]
    rows = xb.shape[0]
    x2 = jnp.concatenate([xb, xb], 0)
    near = jnp.dot(phi_ref[...], x2, preferred_element_type=jnp.float32)
    y = ci_ref[0:1] * near[0:rows]
    for n in range(1, ci_ref.shape[0]):
        y = y + ci_ref[n : n + 1] * near[n * rows : (n + 1) * rows]
    moments = jnp.dot(mom_ref[...], x2, preferred_element_type=jnp.float32)
    z, parts = carry_subblocks(moments, z_ref[...], cs_ref, l16_ref[...], inter_ref)
    z_ref[...] = z
    high, low = split_pair(jnp.concatenate(parts, 0))
    far = jnp.dot(psi_ref[...], jnp.concatenate([high, low, high], 0), preferred_element_type=jnp.float32)
    total = y + far + skip_ref[...] * xb.astype(jnp.float32)
    o_ref[...] = (gate_ref[...].astype(jnp.float32) * total).astype(o_ref.dtype)


def np_split(values):
    high = values.astype(jnp.bfloat16)
    low = (values - high.astype(np.float64)).astype(jnp.bfloat16)
    return high, low


def bases(rows):
    subs = rows // SUB
    n = np.arange(TERMS, dtype=np.float64)
    t = np.arange(rows)
    sb, tl = t // SUB, (t % SUB).astype(np.float64)
    same = sb[:, None] == sb[None, :]
    lag = (t[:, None] - t[None, :]).astype(np.float64)
    near = np.where(
        (same & (lag >= 0))[None], ((lag - 7.5) / 8.0)[None] ** n[:, None, None], 0.0
    ).reshape(TERMS * rows, rows)
    own = np.arange(subs)[:, None] == sb[None, :]
    mom = np.where(own[:, None, :], ((7.5 - tl) / 8.0)[None, None, :] ** n[None, :, None], 0.0)
    mom = mom.reshape(subs * TERMS, rows)
    psi = np.where(own.T[:, :, None], ((tl - 7.5) / 8.0)[:, None, None] ** n[None, None, :], 0.0)
    psi = psi.reshape(rows, subs * TERMS)
    nh, nl = np_split(near)
    mh, ml = np_split(mom)
    ph, pl_ = np_split(psi)
    return (
        jnp.asarray(np.concatenate([nh, nl], 1)),
        jnp.asarray(np.concatenate([mh, ml], 1)),
        jnp.asarray(np.concatenate([ph, ph, pl_], 1)),
    )


def long_conv_out(lr_input, gate0, lr_rate, lr_residue, lr_skip):
    count, chans = lr_input.shape
    modes = lr_rate.shape[1]
    rows = BLOCK
    lanes = min(LANES, chans)
    blocks = count // rows
    rate = lr_rate.T
    weight = lr_residue.T * jnp.sqrt(rate)
    n = jnp.arange(TERMS, dtype=jnp.float32)
    fact = jnp.cumprod(jnp.maximum(n, 1.0))
    powers = (-8.0 * rate)[None] ** n[:, None, None] / fact[:, None, None]
    l75 = jnp.exp(-7.5 * rate)
    cs = l75[None] * powers
    ci = jnp.sum(weight[None] * cs, axis=1)
    inter = ((weight * jnp.exp(-8.5 * rate))[None] * powers).transpose(1, 0, 2)
    l16 = jnp.exp(-float(SUB) * rate)
    phi, mom, psi = bases(rows)
    grid = (chans // lanes, blocks)
    subs_terms = mom.shape[0]
    params = pltpu.CompilerParams(dimension_semantics=("arbitrary", "arbitrary"))

    final = pl.pallas_call(
        state_kernel,
        grid=grid,
        in_specs=[
            pl.BlockSpec((rows, lanes), lambda j, b: (b, j)),
            pl.BlockSpec((subs_terms, 2 * rows), lambda j, b: (0, 0)),
            pl.BlockSpec((TERMS, modes, lanes), lambda j, b: (0, 0, j)),
            pl.BlockSpec((modes, lanes), lambda j, b: (0, j)),
        ],
        out_specs=pl.BlockSpec((modes, lanes), lambda j, b: (0, j)),
        out_shape=jax.ShapeDtypeStruct((modes, chans), jnp.float32),
        scratch_shapes=[pltpu.VMEM((modes, lanes), jnp.float32)],
        compiler_params=params,
    )(lr_input, mom, cs, l16)

    devices = lax.axis_size("ctx")
    incoming = jnp.zeros_like(final)
    for shift in range(1, devices):
        earlier = passed_along(final, "ctx", shift)
        incoming = incoming + jnp.exp(-rate * float((shift - 1) * count)) * earlier

    return pl.pallas_call(
        main_kernel,
        grid=grid,
        in_specs=[
            pl.BlockSpec((rows, lanes), lambda j, b: (b, j)),
            pl.BlockSpec((rows, lanes), lambda j, b: (b, j)),
            pl.BlockSpec((TERMS * rows, 2 * rows), lambda j, b: (0, 0)),
            pl.BlockSpec((subs_terms, 2 * rows), lambda j, b: (0, 0)),
            pl.BlockSpec((rows, 3 * subs_terms), lambda j, b: (0, 0)),
            pl.BlockSpec((TERMS, lanes), lambda j, b: (0, j)),
            pl.BlockSpec((TERMS, modes, lanes), lambda j, b: (0, 0, j)),
            pl.BlockSpec((modes, TERMS, lanes), lambda j, b: (0, 0, j)),
            pl.BlockSpec((modes, lanes), lambda j, b: (0, j)),
            pl.BlockSpec((modes, lanes), lambda j, b: (0, j)),
            pl.BlockSpec((1, lanes), lambda j, b: (0, j)),
        ],
        out_specs=pl.BlockSpec((rows, lanes), lambda j, b: (b, j)),
        out_shape=jax.ShapeDtypeStruct((count, chans), jnp.bfloat16),
        scratch_shapes=[pltpu.VMEM((modes, lanes), jnp.float32)],
        compiler_params=params,
    )(lr_input, gate0, phi, mom, psi, ci, cs, inter, l16, incoming, lr_skip[None, :])


HALO = 144


def front_kernel(feat_ref, halo_ref, sf_ref, rows_ref, gate_ref, o_ref, ext_ref, prod_ref):
    count = feat_ref.shape[1]
    lanes = feat_ref.shape[2]
    groups = rows_ref.shape[0]
    taps = rows_ref.shape[1] // 2
    width = sf_ref.shape[1]
    toep = [
        pltpu.roll(
            jnp.broadcast_to(rows_ref[g : g + 1, :], (taps, 2 * taps)), 0, 1, stride=1, stride_axis=0
        ).astype(jnp.bfloat16)
        for g in range(groups)
    ]
    for i in range(3):
        ext_ref[i, 0:HALO, :] = halo_ref[i].astype(jnp.float32)
        ext_ref[i, HALO : HALO + count, :] = feat_ref[i].astype(jnp.float32)
    taps_row = [[sf_ref[i, j : j + 1, :] for j in range(width)] for i in range(3)]

    def plane(i, e0):
        total = taps_row[i][0] * ext_ref[i, e0 : e0 + taps, :]
        for j in range(1, width):
            total = total + taps_row[i][j] * ext_ref[i, e0 - j : e0 - j + taps, :]
        return total

    lane_group = lax.broadcasted_iota(jnp.int32, (taps, lanes), 1) // (lanes // groups)
    for t0 in range(-taps, count, taps):
        e0 = t0 + HALO
        prod = (plane(1, e0) * plane(2, e0)).astype(jnp.bfloat16)
        prod_ref[e0 : e0 + taps, :] = prod
        if t0 < 0:
            continue
        window = prod_ref[e0 - taps : e0 + taps, :]
        mixed = None
        for g in range(groups):
            res = jnp.dot(toep[g], window, preferred_element_type=jnp.float32)
            mixed = res if mixed is None else jnp.where(lane_group == g, res, mixed)
        query = plane(0, e0)
        gate = gate_ref[t0 : t0 + taps, :].astype(jnp.float32)
        o_ref[t0 : t0 + taps, :] = (gate * query * mixed).astype(o_ref.dtype)


def front(planes, halo, short_filter, mr_filter, gate1):
    _, count, chans = planes.shape
    groups, taps = mr_filter.shape
    lanes = 128
    per_tile = lanes // (chans // groups)
    template = jnp.concatenate(
        [
            jnp.zeros((groups, 1), jnp.float32),
            mr_filter[:, ::-1].astype(jnp.float32),
            jnp.zeros((groups, taps - 1), jnp.float32),
        ],
        1,
    )
    sf = short_filter.transpose(1, 0, 2)
    width = sf.shape[1]
    return pl.pallas_call(
        front_kernel,
        grid=(chans // lanes,),
        in_specs=[
            pl.BlockSpec((3, count, lanes), lambda j: (0, 0, j)),
            pl.BlockSpec((3, HALO, lanes), lambda j: (0, 0, j)),
            pl.BlockSpec((3, width, lanes), lambda j: (0, 0, j)),
            pl.BlockSpec((per_tile, 2 * taps), lambda j: (j, 0)),
            pl.BlockSpec((count, lanes), lambda j: (0, j)),
        ],
        out_specs=pl.BlockSpec((count, lanes), lambda j: (0, j)),
        out_shape=jax.ShapeDtypeStruct((count, chans), jnp.bfloat16),
        scratch_shapes=[
            pltpu.VMEM((3, HALO + count, lanes), jnp.float32),
            pltpu.VMEM((HALO + count, lanes), jnp.bfloat16),
        ],
        compiler_params=pltpu.CompilerParams(dimension_semantics=("arbitrary",)),
    )(planes, halo, sf, template, gate1)


def per_device(features, short_filter, mr_filter, lr_gates, lr_rate, lr_residue, lr_skip):
    count = features.shape[0]
    planes = features.transpose(1, 0, 2)
    halo = passed_along(planes[:, count - HALO :], "ctx", 1)
    gates = lr_gates.transpose(1, 0, 2)
    lr_input = front(planes, halo, short_filter, mr_filter, gates[1])
    return long_conv_out(lr_input, gates[0], lr_rate, lr_residue, lr_skip)


def solution(mesh):
    in_specs = (
        P(("groups", "ctx"), None, ("mp", "sub")),
        P(None, None, ("mp", "sub")),
        P(("mp", "sub"), None),
        P(("groups", "ctx"), None, ("mp", "sub")),
        P(("mp", "sub"), None),
        P(("mp", "sub"), None),
        P(("mp", "sub")),
    )
    out_specs = P(("groups", "ctx"), ("mp", "sub"))
    return jax.shard_map(
        per_device, mesh=mesh, in_specs=in_specs, out_specs=out_specs, check_vma=False
    )
```

```python
import functools

import jax
import numpy as np
import jax.numpy as jnp
from jax import lax
from jax.experimental import pallas as pl
from jax.experimental.pallas import tpu as pltpu
from jax.sharding import PartitionSpec as P

TAPS = 128
SHORT = 7
BLOCK = 128
LANES = 1024


def passed_along(shard, axis, by):
    devices = lax.axis_size(axis)
    pairs = [(i, i + by) for i in range(devices) if 0 <= i + by < devices]
    return lax.ppermute(shard, axis, pairs)


def featurize(extended, weights):
    width = weights.shape[0]
    count = extended.shape[0] - (width - 1)
    total = jnp.zeros((count,) + extended.shape[1:], jnp.float32)
    for j in range(width):
        total = total + weights[j] * extended[width - 1 - j : width - 1 - j + count]
    return total


def medium_mix(extended, filters):
    groups, taps = filters.shape
    rows = extended.shape[0] - (taps - 1)
    chans = extended.shape[1]
    padded = jnp.concatenate([jnp.zeros((1, chans), jnp.bfloat16), extended], 0)
    blocks = rows // taps
    before = padded[:rows].reshape(blocks, taps, chans)
    current = padded[taps:].reshape(blocks, taps, chans)
    window = jnp.concatenate([before, current], 1).reshape(
        blocks, 2 * taps, groups, chans // groups
    )
    window = window.transpose(2, 3, 0, 1)
    lag = jnp.arange(taps)[:, None] + taps - jnp.arange(2 * taps)[None, :]
    pick = (lag[None] == jnp.arange(taps)[:, None, None]).astype(jnp.bfloat16)
    toeplitz = jnp.einsum("gj,jts->gts", filters, pick, preferred_element_type=jnp.float32)
    toeplitz = toeplitz.astype(jnp.bfloat16)
    mixed = jnp.einsum("gts,gkbs->gkbt", toeplitz, window, preferred_element_type=jnp.float32)
    return mixed.transpose(2, 3, 0, 1).reshape(rows, chans)


SUB = 16
TERMS = 8


def split_pair(values):
    high = values.astype(jnp.bfloat16)
    low = (values - high.astype(jnp.float32)).astype(jnp.bfloat16)
    return high, low


def tree_sum(values):
    while len(values) > 1:
        values = [values[i] + values[i + 1] if i + 1 < len(values) else values[i] for i in range(0, len(values), 2)]
    return values[0]


def carry_subblocks(moments, z, cs_ref, l16, inter_ref=None):
    terms = cs_ref.shape[0]
    subs = moments.shape[0] // terms
    coefs = [cs_ref[n] for n in range(terms)]
    accs = [
        tree_sum([coefs[n] * moments[sb * terms + n : sb * terms + n + 1] for n in range(terms)])
        for sb in range(subs)
    ]
    zs = []
    for sb in range(subs):
        zs.append(z)
        z = l16 * z + accs[sb]
    parts = []
    if inter_ref is not None:
        modes = z.shape[0]
        for sb in range(subs):
            parts.append(tree_sum([inter_ref[r] * zs[sb][r : r + 1] for r in range(modes)]))
    return z, parts


def state_kernel(x_ref, mom_ref, cs_ref, l16_ref, f_ref, z_ref):
    b = pl.program_id(1)

    @pl.when(b == 0)
    def _():
        z_ref[...] = jnp.zeros_like(z_ref)

    xb = x_ref[...]
    moments = jnp.dot(mom_ref[...], jnp.concatenate([xb, xb], 0), preferred_element_type=jnp.float32)
    z, _ = carry_subblocks(moments, z_ref[...], cs_ref, l16_ref[...])
    z_ref[...] = z

    @pl.when(b == pl.num_programs(1) - 1)
    def _():
        f_ref[...] = z


def main_kernel(x_ref, gate_ref, phi_ref, mom_ref, psi_ref, ci_ref, cs_ref, inter_ref, l16_ref,
                zin_ref, skip_ref, o_ref, z_ref):
    b = pl.program_id(1)

    @pl.when(b == 0)
    def _():
        z_ref[...] = zin_ref[...]

    xb = x_ref[...]
    rows = xb.shape[0]
    x2 = jnp.concatenate([xb, xb], 0)
    near = jnp.dot(phi_ref[...], x2, preferred_element_type=jnp.float32)
    y = ci_ref[0:1] * near[0:rows]
    for n in range(1, ci_ref.shape[0]):
        y = y + ci_ref[n : n + 1] * near[n * rows : (n + 1) * rows]
    moments = jnp.dot(mom_ref[...], x2, preferred_element_type=jnp.float32)
    z, parts = carry_subblocks(moments, z_ref[...], cs_ref, l16_ref[...], inter_ref)
    z_ref[...] = z
    high, low = split_pair(jnp.concatenate(parts, 0))
    far = jnp.dot(psi_ref[...], jnp.concatenate([high, low, high], 0), preferred_element_type=jnp.float32)
    total = y + far + skip_ref[...] * xb.astype(jnp.float32)
    o_ref[...] = (gate_ref[:, 0, :].astype(jnp.float32) * total).astype(o_ref.dtype)


def np_split(values):
    high = values.astype(jnp.bfloat16)
    low = (values - high.astype(np.float64)).astype(jnp.bfloat16)
    return high, low


def bases(rows):
    subs = rows // SUB
    n = np.arange(TERMS, dtype=np.float64)
    t = np.arange(rows)
    sb, tl = t // SUB, (t % SUB).astype(np.float64)
    same = sb[:, None] == sb[None, :]
    lag = (t[:, None] - t[None, :]).astype(np.float64)
    near = np.where(
        (same & (lag >= 0))[None], ((lag - 7.5) / 8.0)[None] ** n[:, None, None], 0.0
    ).reshape(TERMS * rows, rows)
    own = np.arange(subs)[:, None] == sb[None, :]
    mom = np.where(own[:, None, :], ((7.5 - tl) / 8.0)[None, None, :] ** n[None, :, None], 0.0)
    mom = mom.reshape(subs * TERMS, rows)
    psi = np.where(own.T[:, :, None], ((tl - 7.5) / 8.0)[:, None, None] ** n[None, None, :], 0.0)
    psi = psi.reshape(rows, subs * TERMS)
    nh, nl = np_split(near)
    mh, ml = np_split(mom)
    ph, pl_ = np_split(psi)
    return (
        jnp.asarray(np.concatenate([nh, nl], 1)),
        jnp.asarray(np.concatenate([mh, ml], 1)),
        jnp.asarray(np.concatenate([ph, ph, pl_], 1)),
    )


def long_conv_out(lr_input, gate0, lr_rate, lr_residue, lr_skip):
    count, chans = lr_input.shape
    modes = lr_rate.shape[1]
    rows = BLOCK
    lanes = min(LANES, chans)
    blocks = count // rows
    rate = lr_rate.T
    weight = lr_residue.T * jnp.sqrt(rate)
    n = jnp.arange(TERMS, dtype=jnp.float32)
    fact = jnp.cumprod(jnp.maximum(n, 1.0))
    powers = (-8.0 * rate)[None] ** n[:, None, None] / fact[:, None, None]
    l75 = jnp.exp(-7.5 * rate)
    cs = l75[None] * powers
    ci = jnp.sum(weight[None] * cs, axis=1)
    inter = ((weight * jnp.exp(-8.5 * rate))[None] * powers).transpose(1, 0, 2)
    l16 = jnp.exp(-float(SUB) * rate)
    phi, mom, psi = bases(rows)
    grid = (chans // lanes, blocks)
    subs_terms = mom.shape[0]
    params = pltpu.CompilerParams(dimension_semantics=("arbitrary", "arbitrary"))

    final = pl.pallas_call(
        state_kernel,
        grid=grid,
        in_specs=[
            pl.BlockSpec((rows, lanes), lambda j, b: (b, j)),
            pl.BlockSpec((subs_terms, 2 * rows), lambda j, b: (0, 0)),
            pl.BlockSpec((TERMS, modes, lanes), lambda j, b: (0, 0, j)),
            pl.BlockSpec((modes, lanes), lambda j, b: (0, j)),
        ],
        out_specs=pl.BlockSpec((modes, lanes), lambda j, b: (0, j)),
        out_shape=jax.ShapeDtypeStruct((modes, chans), jnp.float32),
        scratch_shapes=[pltpu.VMEM((modes, lanes), jnp.float32)],
        compiler_params=params,
    )(lr_input, mom, cs, l16)

    devices = lax.axis_size("ctx")
    incoming = jnp.zeros_like(final)
    for shift in range(1, devices):
        earlier = passed_along(final, "ctx", shift)
        incoming = incoming + jnp.exp(-rate * float((shift - 1) * count)) * earlier

    return pl.pallas_call(
        main_kernel,
        grid=grid,
        in_specs=[
            pl.BlockSpec((rows, lanes), lambda j, b: (b, j)),
            pl.BlockSpec((rows, 2, lanes), lambda j, b: (b, 0, j)),
            pl.BlockSpec((TERMS * rows, 2 * rows), lambda j, b: (0, 0)),
            pl.BlockSpec((subs_terms, 2 * rows), lambda j, b: (0, 0)),
            pl.BlockSpec((rows, 3 * subs_terms), lambda j, b: (0, 0)),
            pl.BlockSpec((TERMS, lanes), lambda j, b: (0, j)),
            pl.BlockSpec((TERMS, modes, lanes), lambda j, b: (0, 0, j)),
            pl.BlockSpec((modes, TERMS, lanes), lambda j, b: (0, 0, j)),
            pl.BlockSpec((modes, lanes), lambda j, b: (0, j)),
            pl.BlockSpec((modes, lanes), lambda j, b: (0, j)),
            pl.BlockSpec((1, lanes), lambda j, b: (0, j)),
        ],
        out_specs=pl.BlockSpec((rows, lanes), lambda j, b: (b, j)),
        out_shape=jax.ShapeDtypeStruct((count, chans), jnp.bfloat16),
        scratch_shapes=[pltpu.VMEM((modes, lanes), jnp.float32)],
        compiler_params=params,
    )(lr_input, gate0, phi, mom, psi, ci, cs, inter, l16, incoming, lr_skip[None, :])


HALO = 144


def front_kernel(feat_ref, halo_ref, sf_ref, rows_ref, gate_ref, o_ref, ext_ref, prod_ref):
    count = feat_ref.shape[1]
    lanes = feat_ref.shape[2]
    groups = rows_ref.shape[0]
    taps = rows_ref.shape[1] // 2
    width = sf_ref.shape[1]
    toep = [
        pltpu.roll(
            jnp.broadcast_to(rows_ref[g : g + 1, :], (taps, 2 * taps)), 0, 1, stride=1, stride_axis=0
        ).astype(jnp.bfloat16)
        for g in range(groups)
    ]
    for i in range(3):
        ext_ref[i, 0:HALO, :] = halo_ref[i].astype(jnp.float32)
        ext_ref[i, HALO : HALO + count, :] = feat_ref[i].astype(jnp.float32)
    taps_row = [[sf_ref[i, j : j + 1, :] for j in range(width)] for i in range(3)]

    def plane(i, e0):
        total = taps_row[i][0] * ext_ref[i, e0 : e0 + taps, :]
        for j in range(1, width):
            total = total + taps_row[i][j] * ext_ref[i, e0 - j : e0 - j + taps, :]
        return total

    lane_group = lax.broadcasted_iota(jnp.int32, (taps, lanes), 1) // (lanes // groups)
    for t0 in range(-taps, count, taps):
        e0 = t0 + HALO
        prod = (plane(1, e0) * plane(2, e0)).astype(jnp.bfloat16)
        prod_ref[e0 : e0 + taps, :] = prod
        if t0 < 0:
            continue
        window = prod_ref[e0 - taps : e0 + taps, :]
        mixed = None
        for g in range(groups):
            res = jnp.dot(toep[g], window, preferred_element_type=jnp.float32)
            mixed = res if mixed is None else jnp.where(lane_group == g, res, mixed)
        query = plane(0, e0)
        gate = gate_ref[t0 : t0 + taps, :].astype(jnp.float32)
        o_ref[t0 : t0 + taps, :] = (gate * query * mixed).astype(o_ref.dtype)


def front(planes, halo, short_filter, mr_filter, gate1):
    _, count, chans = planes.shape
    groups, taps = mr_filter.shape
    lanes = 128
    per_tile = lanes // (chans // groups)
    template = jnp.concatenate(
        [
            jnp.zeros((groups, 1), jnp.float32),
            mr_filter[:, ::-1].astype(jnp.float32),
            jnp.zeros((groups, taps - 1), jnp.float32),
        ],
        1,
    )
    sf = short_filter.transpose(1, 0, 2)
    width = sf.shape[1]
    return pl.pallas_call(
        front_kernel,
        grid=(chans // lanes,),
        in_specs=[
            pl.BlockSpec((3, count, lanes), lambda j: (0, 0, j)),
            pl.BlockSpec((3, HALO, lanes), lambda j: (0, 0, j)),
            pl.BlockSpec((3, width, lanes), lambda j: (0, 0, j)),
            pl.BlockSpec((per_tile, 2 * taps), lambda j: (j, 0)),
            pl.BlockSpec((count, lanes), lambda j: (0, j)),
        ],
        out_specs=pl.BlockSpec((count, lanes), lambda j: (0, j)),
        out_shape=jax.ShapeDtypeStruct((count, chans), jnp.bfloat16),
        scratch_shapes=[
            pltpu.VMEM((3, HALO + count, lanes), jnp.float32),
            pltpu.VMEM((HALO + count, lanes), jnp.bfloat16),
        ],
        compiler_params=pltpu.CompilerParams(dimension_semantics=("arbitrary",)),
    )(planes, halo, sf, template, gate1)


def per_device(features, short_filter, mr_filter, lr_gates, lr_rate, lr_residue, lr_skip):
    count = features.shape[0]
    planes = features.transpose(1, 0, 2)
    halo = passed_along(planes[:, count - HALO :], "ctx", 1)
    lr_input = front(planes, halo, short_filter, mr_filter, lr_gates[:, 1, :])
    return long_conv_out(lr_input, lr_gates, lr_rate, lr_residue, lr_skip)


def solution(mesh):
    in_specs = (
        P(("groups", "ctx"), None, ("mp", "sub")),
        P(None, None, ("mp", "sub")),
        P(("mp", "sub"), None),
        P(("groups", "ctx"), None, ("mp", "sub")),
        P(("mp", "sub"), None),
        P(("mp", "sub"), None),
        P(("mp", "sub")),
    )
    out_specs = P(("groups", "ctx"), ("mp", "sub"))
    return jax.shard_map(
        per_device, mesh=mesh, in_specs=in_specs, out_specs=out_specs, check_vma=False
    )
```

```python
import functools

import jax
import numpy as np
import jax.numpy as jnp
from jax import lax
from jax.experimental import pallas as pl
from jax.experimental.pallas import tpu as pltpu
from jax.sharding import PartitionSpec as P

TAPS = 128
SHORT = 7
BLOCK = 256
LANES = 1024


def passed_along(shard, axis, by):
    devices = lax.axis_size(axis)
    pairs = [(i, i + by) for i in range(devices) if 0 <= i + by < devices]
    return lax.ppermute(shard, axis, pairs)


def featurize(extended, weights):
    width = weights.shape[0]
    count = extended.shape[0] - (width - 1)
    total = jnp.zeros((count,) + extended.shape[1:], jnp.float32)
    for j in range(width):
        total = total + weights[j] * extended[width - 1 - j : width - 1 - j + count]
    return total


def medium_mix(extended, filters):
    groups, taps = filters.shape
    rows = extended.shape[0] - (taps - 1)
    chans = extended.shape[1]
    padded = jnp.concatenate([jnp.zeros((1, chans), jnp.bfloat16), extended], 0)
    blocks = rows // taps
    before = padded[:rows].reshape(blocks, taps, chans)
    current = padded[taps:].reshape(blocks, taps, chans)
    window = jnp.concatenate([before, current], 1).reshape(
        blocks, 2 * taps, groups, chans // groups
    )
    window = window.transpose(2, 3, 0, 1)
    lag = jnp.arange(taps)[:, None] + taps - jnp.arange(2 * taps)[None, :]
    pick = (lag[None] == jnp.arange(taps)[:, None, None]).astype(jnp.bfloat16)
    toeplitz = jnp.einsum("gj,jts->gts", filters, pick, preferred_element_type=jnp.float32)
    toeplitz = toeplitz.astype(jnp.bfloat16)
    mixed = jnp.einsum("gts,gkbs->gkbt", toeplitz, window, preferred_element_type=jnp.float32)
    return mixed.transpose(2, 3, 0, 1).reshape(rows, chans)


SUB = 16
TERMS = 8


def split_pair(values):
    high = values.astype(jnp.bfloat16)
    low = (values - high.astype(jnp.float32)).astype(jnp.bfloat16)
    return high, low


def tree_sum(values):
    while len(values) > 1:
        values = [values[i] + values[i + 1] if i + 1 < len(values) else values[i] for i in range(0, len(values), 2)]
    return values[0]


def carry_subblocks(moments, z, cs_ref, l16, inter_ref=None):
    terms = cs_ref.shape[0]
    subs = moments.shape[0] // terms
    coefs = [cs_ref[n] for n in range(terms)]
    accs = [
        tree_sum([coefs[n] * moments[sb * terms + n : sb * terms + n + 1] for n in range(terms)])
        for sb in range(subs)
    ]
    zs = []
    for sb in range(subs):
        zs.append(z)
        z = l16 * z + accs[sb]
    parts = []
    if inter_ref is not None:
        modes = z.shape[0]
        for sb in range(subs):
            parts.append(tree_sum([inter_ref[r] * zs[sb][r : r + 1] for r in range(modes)]))
    return z, parts


def state_kernel(x_ref, mom_ref, cs_ref, l16_ref, f_ref, z_ref):
    b = pl.program_id(1)

    @pl.when(b == 0)
    def _():
        z_ref[...] = jnp.zeros_like(z_ref)

    xb = x_ref[...]
    moments = jnp.dot(mom_ref[...], jnp.concatenate([xb, xb], 0), preferred_element_type=jnp.float32)
    z, _ = carry_subblocks(moments, z_ref[...], cs_ref, l16_ref[...])
    z_ref[...] = z

    @pl.when(b == pl.num_programs(1) - 1)
    def _():
        f_ref[...] = z


def main_kernel(x_ref, gate_ref, phi_ref, mom_ref, psi_ref, ci_ref, cs_ref, inter_ref, l16_ref,
                zin_ref, skip_ref, o_ref, z_ref):
    b = pl.program_id(1)

    @pl.when(b == 0)
    def _():
        z_ref[...] = zin_ref[...]

    xb = x_ref[...]
    rows = xb.shape[0]
    x2 = jnp.concatenate([xb, xb], 0)
    near = jnp.dot(phi_ref[...], x2, preferred_element_type=jnp.float32)
    y = ci_ref[0:1] * near[0:rows]
    for n in range(1, ci_ref.shape[0]):
        y = y + ci_ref[n : n + 1] * near[n * rows : (n + 1) * rows]
    moments = jnp.dot(mom_ref[...], x2, preferred_element_type=jnp.float32)
    z, parts = carry_subblocks(moments, z_ref[...], cs_ref, l16_ref[...], inter_ref)
    z_ref[...] = z
    high, low = split_pair(jnp.concatenate(parts, 0))
    far = jnp.dot(psi_ref[...], jnp.concatenate([high, low, high], 0), preferred_element_type=jnp.float32)
    total = y + far + skip_ref[...] * xb.astype(jnp.float32)
    o_ref[...] = (gate_ref[...].astype(jnp.float32) * total).astype(o_ref.dtype)


def np_split(values):
    high = values.astype(jnp.bfloat16)
    low = (values - high.astype(np.float64)).astype(jnp.bfloat16)
    return high, low


def bases(rows):
    subs = rows // SUB
    n = np.arange(TERMS, dtype=np.float64)
    t = np.arange(rows)
    sb, tl = t // SUB, (t % SUB).astype(np.float64)
    same = sb[:, None] == sb[None, :]
    lag = (t[:, None] - t[None, :]).astype(np.float64)
    near = np.where(
        (same & (lag >= 0))[None], ((lag - 7.5) / 8.0)[None] ** n[:, None, None], 0.0
    ).reshape(TERMS * rows, rows)
    own = np.arange(subs)[:, None] == sb[None, :]
    mom = np.where(own[:, None, :], ((7.5 - tl) / 8.0)[None, None, :] ** n[None, :, None], 0.0)
    mom = mom.reshape(subs * TERMS, rows)
    psi = np.where(own.T[:, :, None], ((tl - 7.5) / 8.0)[:, None, None] ** n[None, None, :], 0.0)
    psi = psi.reshape(rows, subs * TERMS)
    nh, nl = np_split(near)
    mh, ml = np_split(mom)
    ph, pl_ = np_split(psi)
    return (
        jnp.asarray(np.concatenate([nh, nl], 1)),
        jnp.asarray(np.concatenate([mh, ml], 1)),
        jnp.asarray(np.concatenate([ph, ph, pl_], 1)),
    )


def long_conv_out(lr_input, gate0, lr_rate, lr_residue, lr_skip):
    count, chans = lr_input.shape
    modes = lr_rate.shape[1]
    rows = BLOCK
    lanes = min(LANES, chans)
    blocks = count // rows
    rate = lr_rate.T
    weight = lr_residue.T * jnp.sqrt(rate)
    n = jnp.arange(TERMS, dtype=jnp.float32)
    fact = jnp.cumprod(jnp.maximum(n, 1.0))
    powers = (-8.0 * rate)[None] ** n[:, None, None] / fact[:, None, None]
    l75 = jnp.exp(-7.5 * rate)
    cs = l75[None] * powers
    ci = jnp.sum(weight[None] * cs, axis=1)
    inter = ((weight * jnp.exp(-8.5 * rate))[None] * powers).transpose(1, 0, 2)
    l16 = jnp.exp(-float(SUB) * rate)
    phi, mom, psi = bases(rows)
    grid = (chans // lanes, blocks)
    subs_terms = mom.shape[0]
    params = pltpu.CompilerParams(dimension_semantics=("arbitrary", "arbitrary"))

    final = pl.pallas_call(
        state_kernel,
        grid=grid,
        in_specs=[
            pl.BlockSpec((rows, lanes), lambda j, b: (b, j)),
            pl.BlockSpec((subs_terms, 2 * rows), lambda j, b: (0, 0)),
            pl.BlockSpec((TERMS, modes, lanes), lambda j, b: (0, 0, j)),
            pl.BlockSpec((modes, lanes), lambda j, b: (0, j)),
        ],
        out_specs=pl.BlockSpec((modes, lanes), lambda j, b: (0, j)),
        out_shape=jax.ShapeDtypeStruct((modes, chans), jnp.float32),
        scratch_shapes=[pltpu.VMEM((modes, lanes), jnp.float32)],
        compiler_params=params,
    )(lr_input, mom, cs, l16)

    devices = lax.axis_size("ctx")
    incoming = jnp.zeros_like(final)
    for shift in range(1, devices):
        earlier = passed_along(final, "ctx", shift)
        incoming = incoming + jnp.exp(-rate * float((shift - 1) * count)) * earlier

    return pl.pallas_call(
        main_kernel,
        grid=grid,
        in_specs=[
            pl.BlockSpec((rows, lanes), lambda j, b: (b, j)),
            pl.BlockSpec((rows, lanes), lambda j, b: (b, j)),
            pl.BlockSpec((TERMS * rows, 2 * rows), lambda j, b: (0, 0)),
            pl.BlockSpec((subs_terms, 2 * rows), lambda j, b: (0, 0)),
            pl.BlockSpec((rows, 3 * subs_terms), lambda j, b: (0, 0)),
            pl.BlockSpec((TERMS, lanes), lambda j, b: (0, j)),
            pl.BlockSpec((TERMS, modes, lanes), lambda j, b: (0, 0, j)),
            pl.BlockSpec((modes, TERMS, lanes), lambda j, b: (0, 0, j)),
            pl.BlockSpec((modes, lanes), lambda j, b: (0, j)),
            pl.BlockSpec((modes, lanes), lambda j, b: (0, j)),
            pl.BlockSpec((1, lanes), lambda j, b: (0, j)),
        ],
        out_specs=pl.BlockSpec((rows, lanes), lambda j, b: (b, j)),
        out_shape=jax.ShapeDtypeStruct((count, chans), jnp.bfloat16),
        scratch_shapes=[pltpu.VMEM((modes, lanes), jnp.float32)],
        compiler_params=params,
    )(lr_input, gate0, phi, mom, psi, ci, cs, inter, l16, incoming, lr_skip[None, :])


HALO = 144


def front_kernel(feat_ref, halo_ref, sf_ref, rows_ref, gate_ref, o_ref, ext_ref, prod_ref):
    count = feat_ref.shape[1]
    lanes = feat_ref.shape[2]
    groups = rows_ref.shape[0]
    taps = rows_ref.shape[1] // 2
    width = sf_ref.shape[1]
    toep = [
        pltpu.roll(
            jnp.broadcast_to(rows_ref[g : g + 1, :], (taps, 2 * taps)), 0, 1, stride=1, stride_axis=0
        ).astype(jnp.bfloat16)
        for g in range(groups)
    ]
    for i in range(3):
        ext_ref[i, 0:HALO, :] = halo_ref[i].astype(jnp.float32)
        ext_ref[i, HALO : HALO + count, :] = feat_ref[i].astype(jnp.float32)
    taps_row = [[sf_ref[i, j : j + 1, :] for j in range(width)] for i in range(3)]

    def plane(i, e0):
        total = taps_row[i][0] * ext_ref[i, e0 : e0 + taps, :]
        for j in range(1, width):
            total = total + taps_row[i][j] * ext_ref[i, e0 - j : e0 - j + taps, :]
        return total

    lane_group = lax.broadcasted_iota(jnp.int32, (taps, lanes), 1) // (lanes // groups)
    for t0 in range(-taps, count, taps):
        e0 = t0 + HALO
        prod = (plane(1, e0) * plane(2, e0)).astype(jnp.bfloat16)
        prod_ref[e0 : e0 + taps, :] = prod
        if t0 < 0:
            continue
        window = prod_ref[e0 - taps : e0 + taps, :]
        mixed = None
        for g in range(groups):
            res = jnp.dot(toep[g], window, preferred_element_type=jnp.float32)
            mixed = res if mixed is None else jnp.where(lane_group == g, res, mixed)
        query = plane(0, e0)
        gate = gate_ref[t0 : t0 + taps, :].astype(jnp.float32)
        o_ref[t0 : t0 + taps, :] = (gate * query * mixed).astype(o_ref.dtype)


def front(planes, halo, short_filter, mr_filter, gate1):
    _, count, chans = planes.shape
    groups, taps = mr_filter.shape
    lanes = 128
    per_tile = lanes // (chans // groups)
    template = jnp.concatenate(
        [
            jnp.zeros((groups, 1), jnp.float32),
            mr_filter[:, ::-1].astype(jnp.float32),
            jnp.zeros((groups, taps - 1), jnp.float32),
        ],
        1,
    )
    sf = short_filter.transpose(1, 0, 2)
    width = sf.shape[1]
    return pl.pallas_call(
        front_kernel,
        grid=(chans // lanes,),
        in_specs=[
            pl.BlockSpec((3, count, lanes), lambda j: (0, 0, j)),
            pl.BlockSpec((3, HALO, lanes), lambda j: (0, 0, j)),
            pl.BlockSpec((3, width, lanes), lambda j: (0, 0, j)),
            pl.BlockSpec((per_tile, 2 * taps), lambda j: (j, 0)),
            pl.BlockSpec((count, lanes), lambda j: (0, j)),
        ],
        out_specs=pl.BlockSpec((count, lanes), lambda j: (0, j)),
        out_shape=jax.ShapeDtypeStruct((count, chans), jnp.bfloat16),
        scratch_shapes=[
            pltpu.VMEM((3, HALO + count, lanes), jnp.float32),
            pltpu.VMEM((HALO + count, lanes), jnp.bfloat16),
        ],
        compiler_params=pltpu.CompilerParams(dimension_semantics=("arbitrary",)),
    )(planes, halo, sf, template, gate1)


def per_device(features, short_filter, mr_filter, lr_gates, lr_rate, lr_residue, lr_skip):
    count = features.shape[0]
    planes = features.transpose(1, 0, 2)
    halo = passed_along(planes[:, count - HALO :], "ctx", 1)
    gates = lr_gates.transpose(1, 0, 2)
    lr_input = front(planes, halo, short_filter, mr_filter, gates[1])
    return long_conv_out(lr_input, gates[0], lr_rate, lr_residue, lr_skip)


def solution(mesh):
    in_specs = (
        P(("groups", "ctx"), None, ("mp", "sub")),
        P(None, None, ("mp", "sub")),
        P(("mp", "sub"), None),
        P(("groups", "ctx"), None, ("mp", "sub")),
        P(("mp", "sub"), None),
        P(("mp", "sub"), None),
        P(("mp", "sub")),
    )
    out_specs = P(("groups", "ctx"), ("mp", "sub"))
    return jax.shard_map(
        per_device, mesh=mesh, in_specs=in_specs, out_specs=out_specs, check_vma=False
    )
```

```python
import functools

import jax
import numpy as np
import jax.numpy as jnp
from jax import lax
from jax.experimental import pallas as pl
from jax.experimental.pallas import tpu as pltpu
from jax.sharding import PartitionSpec as P

TAPS = 128
SHORT = 7
BLOCK = 128
STATE_BLOCK = 256
LANES = 1024


def passed_along(shard, axis, by):
    devices = lax.axis_size(axis)
    pairs = [(i, i + by) for i in range(devices) if 0 <= i + by < devices]
    return lax.ppermute(shard, axis, pairs)


def featurize(extended, weights):
    width = weights.shape[0]
    count = extended.shape[0] - (width - 1)
    total = jnp.zeros((count,) + extended.shape[1:], jnp.float32)
    for j in range(width):
        total = total + weights[j] * extended[width - 1 - j : width - 1 - j + count]
    return total


def medium_mix(extended, filters):
    groups, taps = filters.shape
    rows = extended.shape[0] - (taps - 1)
    chans = extended.shape[1]
    padded = jnp.concatenate([jnp.zeros((1, chans), jnp.bfloat16), extended], 0)
    blocks = rows // taps
    before = padded[:rows].reshape(blocks, taps, chans)
    current = padded[taps:].reshape(blocks, taps, chans)
    window = jnp.concatenate([before, current], 1).reshape(
        blocks, 2 * taps, groups, chans // groups
    )
    window = window.transpose(2, 3, 0, 1)
    lag = jnp.arange(taps)[:, None] + taps - jnp.arange(2 * taps)[None, :]
    pick = (lag[None] == jnp.arange(taps)[:, None, None]).astype(jnp.bfloat16)
    toeplitz = jnp.einsum("gj,jts->gts", filters, pick, preferred_element_type=jnp.float32)
    toeplitz = toeplitz.astype(jnp.bfloat16)
    mixed = jnp.einsum("gts,gkbs->gkbt", toeplitz, window, preferred_element_type=jnp.float32)
    return mixed.transpose(2, 3, 0, 1).reshape(rows, chans)


SUB = 16
TERMS = 8


def split_pair(values):
    high = values.astype(jnp.bfloat16)
    low = (values - high.astype(jnp.float32)).astype(jnp.bfloat16)
    return high, low


def tree_sum(values):
    while len(values) > 1:
        values = [values[i] + values[i + 1] if i + 1 < len(values) else values[i] for i in range(0, len(values), 2)]
    return values[0]


def carry_subblocks(moments, z, cs_ref, l16, inter_ref=None):
    terms = cs_ref.shape[0]
    subs = moments.shape[0] // terms
    coefs = [cs_ref[n] for n in range(terms)]
    accs = [
        tree_sum([coefs[n] * moments[sb * terms + n : sb * terms + n + 1] for n in range(terms)])
        for sb in range(subs)
    ]
    zs = []
    for sb in range(subs):
        zs.append(z)
        z = l16 * z + accs[sb]
    parts = []
    if inter_ref is not None:
        modes = z.shape[0]
        for sb in range(subs):
            parts.append(tree_sum([inter_ref[r] * zs[sb][r : r + 1] for r in range(modes)]))
    return z, parts


def state_kernel(x_ref, mom_ref, cs_ref, l16_ref, f_ref, z_ref):
    b = pl.program_id(1)

    @pl.when(b == 0)
    def _():
        z_ref[...] = jnp.zeros_like(z_ref)

    xb = x_ref[...]
    moments = jnp.dot(mom_ref[...], jnp.concatenate([xb, xb], 0), preferred_element_type=jnp.float32)
    z, _ = carry_subblocks(moments, z_ref[...], cs_ref, l16_ref[...])
    z_ref[...] = z

    @pl.when(b == pl.num_programs(1) - 1)
    def _():
        f_ref[...] = z


def main_kernel(x_ref, gate_ref, phi_ref, mom_ref, psi_ref, ci_ref, cs_ref, inter_ref, l16_ref,
                zin_ref, skip_ref, o_ref, z_ref):
    b = pl.program_id(1)

    @pl.when(b == 0)
    def _():
        z_ref[...] = zin_ref[...]

    xb = x_ref[...]
    rows = xb.shape[0]
    x2 = jnp.concatenate([xb, xb], 0)
    near = jnp.dot(phi_ref[...], x2, preferred_element_type=jnp.float32)
    y = ci_ref[0:1] * near[0:rows]
    for n in range(1, ci_ref.shape[0]):
        y = y + ci_ref[n : n + 1] * near[n * rows : (n + 1) * rows]
    moments = jnp.dot(mom_ref[...], x2, preferred_element_type=jnp.float32)
    z, parts = carry_subblocks(moments, z_ref[...], cs_ref, l16_ref[...], inter_ref)
    z_ref[...] = z
    high, low = split_pair(jnp.concatenate(parts, 0))
    far = jnp.dot(psi_ref[...], jnp.concatenate([high, low, high], 0), preferred_element_type=jnp.float32)
    total = y + far + skip_ref[...] * xb.astype(jnp.float32)
    o_ref[...] = (gate_ref[...].astype(jnp.float32) * total).astype(o_ref.dtype)


def np_split(values):
    high = values.astype(jnp.bfloat16)
    low = (values - high.astype(np.float64)).astype(jnp.bfloat16)
    return high, low


def bases(rows):
    subs = rows // SUB
    n = np.arange(TERMS, dtype=np.float64)
    t = np.arange(rows)
    sb, tl = t // SUB, (t % SUB).astype(np.float64)
    same = sb[:, None] == sb[None, :]
    lag = (t[:, None] - t[None, :]).astype(np.float64)
    near = np.where(
        (same & (lag >= 0))[None], ((lag - 7.5) / 8.0)[None] ** n[:, None, None], 0.0
    ).reshape(TERMS * rows, rows)
    own = np.arange(subs)[:, None] == sb[None, :]
    mom = np.where(own[:, None, :], ((7.5 - tl) / 8.0)[None, None, :] ** n[None, :, None], 0.0)
    mom = mom.reshape(subs * TERMS, rows)
    psi = np.where(own.T[:, :, None], ((tl - 7.5) / 8.0)[:, None, None] ** n[None, None, :], 0.0)
    psi = psi.reshape(rows, subs * TERMS)
    nh, nl = np_split(near)
    mh, ml = np_split(mom)
    ph, pl_ = np_split(psi)
    return (
        jnp.asarray(np.concatenate([nh, nl], 1)),
        jnp.asarray(np.concatenate([mh, ml], 1)),
        jnp.asarray(np.concatenate([ph, ph, pl_], 1)),
    )


def long_conv_out(lr_input, gate0, lr_rate, lr_residue, lr_skip):
    count, chans = lr_input.shape
    modes = lr_rate.shape[1]
    rows = BLOCK
    lanes = min(LANES, chans)
    blocks = count // rows
    rate = lr_rate.T
    weight = lr_residue.T * jnp.sqrt(rate)
    n = jnp.arange(TERMS, dtype=jnp.float32)
    fact = jnp.cumprod(jnp.maximum(n, 1.0))
    powers = (-8.0 * rate)[None] ** n[:, None, None] / fact[:, None, None]
    l75 = jnp.exp(-7.5 * rate)
    cs = l75[None] * powers
    ci = jnp.sum(weight[None] * cs, axis=1)
    inter = ((weight * jnp.exp(-8.5 * rate))[None] * powers).transpose(1, 0, 2)
    l16 = jnp.exp(-float(SUB) * rate)
    phi, mom, psi = bases(rows)
    grid = (chans // lanes, blocks)
    subs_terms = mom.shape[0]
    params = pltpu.CompilerParams(dimension_semantics=("arbitrary", "arbitrary"))

    wide = min(STATE_BLOCK, count)
    _, mom_wide, _ = bases(wide)
    final = pl.pallas_call(
        state_kernel,
        grid=(chans // lanes, count // wide),
        in_specs=[
            pl.BlockSpec((wide, lanes), lambda j, b: (b, j)),
            pl.BlockSpec(mom_wide.shape, lambda j, b: (0, 0)),
            pl.BlockSpec((TERMS, modes, lanes), lambda j, b: (0, 0, j)),
            pl.BlockSpec((modes, lanes), lambda j, b: (0, j)),
        ],
        out_specs=pl.BlockSpec((modes, lanes), lambda j, b: (0, j)),
        out_shape=jax.ShapeDtypeStruct((modes, chans), jnp.float32),
        scratch_shapes=[pltpu.VMEM((modes, lanes), jnp.float32)],
        compiler_params=params,
    )(lr_input, mom_wide, cs, l16)

    devices = lax.axis_size("ctx")
    incoming = jnp.zeros_like(final)
    for shift in range(1, devices):
        earlier = passed_along(final, "ctx", shift)
        incoming = incoming + jnp.exp(-rate * float((shift - 1) * count)) * earlier

    return pl.pallas_call(
        main_kernel,
        grid=grid,
        in_specs=[
            pl.BlockSpec((rows, lanes), lambda j, b: (b, j)),
            pl.BlockSpec((rows, lanes), lambda j, b: (b, j)),
            pl.BlockSpec((TERMS * rows, 2 * rows), lambda j, b: (0, 0)),
            pl.BlockSpec((subs_terms, 2 * rows), lambda j, b: (0, 0)),
            pl.BlockSpec((rows, 3 * subs_terms), lambda j, b: (0, 0)),
            pl.BlockSpec((TERMS, lanes), lambda j, b: (0, j)),
            pl.BlockSpec((TERMS, modes, lanes), lambda j, b: (0, 0, j)),
            pl.BlockSpec((modes, TERMS, lanes), lambda j, b: (0, 0, j)),
            pl.BlockSpec((modes, lanes), lambda j, b: (0, j)),
            pl.BlockSpec((modes, lanes), lambda j, b: (0, j)),
            pl.BlockSpec((1, lanes), lambda j, b: (0, j)),
        ],
        out_specs=pl.BlockSpec((rows, lanes), lambda j, b: (b, j)),
        out_shape=jax.ShapeDtypeStruct((count, chans), jnp.bfloat16),
        scratch_shapes=[pltpu.VMEM((modes, lanes), jnp.float32)],
        compiler_params=params,
    )(lr_input, gate0, phi, mom, psi, ci, cs, inter, l16, incoming, lr_skip[None, :])


HALO = 144


def front_kernel(feat_ref, halo_ref, sf_ref, rows_ref, gate_ref, o_ref, ext_ref, prod_ref):
    count = feat_ref.shape[1]
    lanes = feat_ref.shape[2]
    groups = rows_ref.shape[0]
    taps = rows_ref.shape[1] // 2
    width = sf_ref.shape[1]
    toep = [
        pltpu.roll(
            jnp.broadcast_to(rows_ref[g : g + 1, :], (taps, 2 * taps)), 0, 1, stride=1, stride_axis=0
        ).astype(jnp.bfloat16)
        for g in range(groups)
    ]
    for i in range(3):
        ext_ref[i, 0:HALO, :] = halo_ref[i].astype(jnp.float32)
        ext_ref[i, HALO : HALO + count, :] = feat_ref[i].astype(jnp.float32)
    taps_row = [[sf_ref[i, j : j + 1, :] for j in range(width)] for i in range(3)]

    def plane(i, e0):
        total = taps_row[i][0] * ext_ref[i, e0 : e0 + taps, :]
        for j in range(1, width):
            total = total + taps_row[i][j] * ext_ref[i, e0 - j : e0 - j + taps, :]
        return total

    lane_group = lax.broadcasted_iota(jnp.int32, (taps, lanes), 1) // (lanes // groups)
    for t0 in range(-taps, count, taps):
        e0 = t0 + HALO
        prod = (plane(1, e0) * plane(2, e0)).astype(jnp.bfloat16)
        prod_ref[e0 : e0 + taps, :] = prod
        if t0 < 0:
            continue
        window = prod_ref[e0 - taps : e0 + taps, :]
        mixed = None
        for g in range(groups):
            res = jnp.dot(toep[g], window, preferred_element_type=jnp.float32)
            mixed = res if mixed is None else jnp.where(lane_group == g, res, mixed)
        query = plane(0, e0)
        gate = gate_ref[t0 : t0 + taps, :].astype(jnp.float32)
        o_ref[t0 : t0 + taps, :] = (gate * query * mixed).astype(o_ref.dtype)


def front(planes, halo, short_filter, mr_filter, gate1):
    _, count, chans = planes.shape
    groups, taps = mr_filter.shape
    lanes = 128
    per_tile = lanes // (chans // groups)
    template = jnp.concatenate(
        [
            jnp.zeros((groups, 1), jnp.float32),
            mr_filter[:, ::-1].astype(jnp.float32),
            jnp.zeros((groups, taps - 1), jnp.float32),
        ],
        1,
    )
    sf = short_filter.transpose(1, 0, 2)
    width = sf.shape[1]
    return pl.pallas_call(
        front_kernel,
        grid=(chans // lanes,),
        in_specs=[
            pl.BlockSpec((3, count, lanes), lambda j: (0, 0, j)),
            pl.BlockSpec((3, HALO, lanes), lambda j: (0, 0, j)),
            pl.BlockSpec((3, width, lanes), lambda j: (0, 0, j)),
            pl.BlockSpec((per_tile, 2 * taps), lambda j: (j, 0)),
            pl.BlockSpec((count, lanes), lambda j: (0, j)),
        ],
        out_specs=pl.BlockSpec((count, lanes), lambda j: (0, j)),
        out_shape=jax.ShapeDtypeStruct((count, chans), jnp.bfloat16),
        scratch_shapes=[
            pltpu.VMEM((3, HALO + count, lanes), jnp.float32),
            pltpu.VMEM((HALO + count, lanes), jnp.bfloat16),
        ],
        compiler_params=pltpu.CompilerParams(dimension_semantics=("arbitrary",)),
    )(planes, halo, sf, template, gate1)


def per_device(features, short_filter, mr_filter, lr_gates, lr_rate, lr_residue, lr_skip):
    count = features.shape[0]
    planes = features.transpose(1, 0, 2)
    halo = passed_along(planes[:, count - HALO :], "ctx", 1)
    gates = lr_gates.transpose(1, 0, 2)
    lr_input = front(planes, halo, short_filter, mr_filter, gates[1])
    return long_conv_out(lr_input, gates[0], lr_rate, lr_residue, lr_skip)


def solution(mesh):
    in_specs = (
        P(("groups", "ctx"), None, ("mp", "sub")),
        P(None, None, ("mp", "sub")),
        P(("mp", "sub"), None),
        P(("groups", "ctx"), None, ("mp", "sub")),
        P(("mp", "sub"), None),
        P(("mp", "sub"), None),
        P(("mp", "sub")),
    )
    out_specs = P(("groups", "ctx"), ("mp", "sub"))
    return jax.shard_map(
        per_device, mesh=mesh, in_specs=in_specs, out_specs=out_specs, check_vma=False
    )
```

```python
import functools

import jax
import numpy as np
import jax.numpy as jnp
from jax import lax
from jax.experimental import pallas as pl
from jax.experimental.pallas import tpu as pltpu
from jax.sharding import PartitionSpec as P

TAPS = 128
SHORT = 7
BLOCK = 128
STATE_BLOCK = 512
LANES = 1024


def passed_along(shard, axis, by):
    devices = lax.axis_size(axis)
    pairs = [(i, i + by) for i in range(devices) if 0 <= i + by < devices]
    return lax.ppermute(shard, axis, pairs)


def featurize(extended, weights):
    width = weights.shape[0]
    count = extended.shape[0] - (width - 1)
    total = jnp.zeros((count,) + extended.shape[1:], jnp.float32)
    for j in range(width):
        total = total + weights[j] * extended[width - 1 - j : width - 1 - j + count]
    return total


def medium_mix(extended, filters):
    groups, taps = filters.shape
    rows = extended.shape[0] - (taps - 1)
    chans = extended.shape[1]
    padded = jnp.concatenate([jnp.zeros((1, chans), jnp.bfloat16), extended], 0)
    blocks = rows // taps
    before = padded[:rows].reshape(blocks, taps, chans)
    current = padded[taps:].reshape(blocks, taps, chans)
    window = jnp.concatenate([before, current], 1).reshape(
        blocks, 2 * taps, groups, chans // groups
    )
    window = window.transpose(2, 3, 0, 1)
    lag = jnp.arange(taps)[:, None] + taps - jnp.arange(2 * taps)[None, :]
    pick = (lag[None] == jnp.arange(taps)[:, None, None]).astype(jnp.bfloat16)
    toeplitz = jnp.einsum("gj,jts->gts", filters, pick, preferred_element_type=jnp.float32)
    toeplitz = toeplitz.astype(jnp.bfloat16)
    mixed = jnp.einsum("gts,gkbs->gkbt", toeplitz, window, preferred_element_type=jnp.float32)
    return mixed.transpose(2, 3, 0, 1).reshape(rows, chans)


SUB = 16
TERMS = 8


def split_pair(values):
    high = values.astype(jnp.bfloat16)
    low = (values - high.astype(jnp.float32)).astype(jnp.bfloat16)
    return high, low


def tree_sum(values):
    while len(values) > 1:
        values = [values[i] + values[i + 1] if i + 1 < len(values) else values[i] for i in range(0, len(values), 2)]
    return values[0]


def carry_subblocks(moments, z, cs_ref, l16, inter_ref=None):
    terms = cs_ref.shape[0]
    subs = moments.shape[0] // terms
    coefs = [cs_ref[n] for n in range(terms)]
    accs = [
        tree_sum([coefs[n] * moments[sb * terms + n : sb * terms + n + 1] for n in range(terms)])
        for sb in range(subs)
    ]
    zs = []
    for sb in range(subs):
        zs.append(z)
        z = l16 * z + accs[sb]
    parts = []
    if inter_ref is not None:
        modes = z.shape[0]
        for sb in range(subs):
            parts.append(tree_sum([inter_ref[r] * zs[sb][r : r + 1] for r in range(modes)]))
    return z, parts


def state_kernel(x_ref, mom_ref, cs_ref, l16_ref, f_ref, z_ref):
    b = pl.program_id(1)

    @pl.when(b == 0)
    def _():
        z_ref[...] = jnp.zeros_like(z_ref)

    xb = x_ref[...]
    moments = jnp.dot(mom_ref[...], jnp.concatenate([xb, xb], 0), preferred_element_type=jnp.float32)
    z, _ = carry_subblocks(moments, z_ref[...], cs_ref, l16_ref[...])
    z_ref[...] = z

    @pl.when(b == pl.num_programs(1) - 1)
    def _():
        f_ref[...] = z


def main_kernel(x_ref, gate_ref, phi_ref, mom_ref, psi_ref, ci_ref, cs_ref, inter_ref, l16_ref,
                zin_ref, skip_ref, o_ref, z_ref):
    b = pl.program_id(1)

    @pl.when(b == 0)
    def _():
        z_ref[...] = zin_ref[...]

    xb = x_ref[...]
    rows = xb.shape[0]
    x2 = jnp.concatenate([xb, xb], 0)
    near = jnp.dot(phi_ref[...], x2, preferred_element_type=jnp.float32)
    y = ci_ref[0:1] * near[0:rows]
    for n in range(1, ci_ref.shape[0]):
        y = y + ci_ref[n : n + 1] * near[n * rows : (n + 1) * rows]
    moments = jnp.dot(mom_ref[...], x2, preferred_element_type=jnp.float32)
    z, parts = carry_subblocks(moments, z_ref[...], cs_ref, l16_ref[...], inter_ref)
    z_ref[...] = z
    high, low = split_pair(jnp.concatenate(parts, 0))
    far = jnp.dot(psi_ref[...], jnp.concatenate([high, low, high], 0), preferred_element_type=jnp.float32)
    total = y + far + skip_ref[...] * xb.astype(jnp.float32)
    o_ref[...] = (gate_ref[...].astype(jnp.float32) * total).astype(o_ref.dtype)


def np_split(values):
    high = values.astype(jnp.bfloat16)
    low = (values - high.astype(np.float64)).astype(jnp.bfloat16)
    return high, low


def bases(rows):
    subs = rows // SUB
    n = np.arange(TERMS, dtype=np.float64)
    t = np.arange(rows)
    sb, tl = t // SUB, (t % SUB).astype(np.float64)
    same = sb[:, None] == sb[None, :]
    lag = (t[:, None] - t[None, :]).astype(np.float64)
    near = np.where(
        (same & (lag >= 0))[None], ((lag - 7.5) / 8.0)[None] ** n[:, None, None], 0.0
    ).reshape(TERMS * rows, rows)
    own = np.arange(subs)[:, None] == sb[None, :]
    mom = np.where(own[:, None, :], ((7.5 - tl) / 8.0)[None, None, :] ** n[None, :, None], 0.0)
    mom = mom.reshape(subs * TERMS, rows)
    psi = np.where(own.T[:, :, None], ((tl - 7.5) / 8.0)[:, None, None] ** n[None, None, :], 0.0)
    psi = psi.reshape(rows, subs * TERMS)
    nh, nl = np_split(near)
    mh, ml = np_split(mom)
    ph, pl_ = np_split(psi)
    return (
        jnp.asarray(np.concatenate([nh, nl], 1)),
        jnp.asarray(np.concatenate([mh, ml], 1)),
        jnp.asarray(np.concatenate([ph, ph, pl_], 1)),
    )


def long_conv_out(lr_input, gate0, lr_rate, lr_residue, lr_skip):
    count, chans = lr_input.shape
    modes = lr_rate.shape[1]
    rows = BLOCK
    lanes = min(LANES, chans)
    blocks = count // rows
    rate = lr_rate.T
    weight = lr_residue.T * jnp.sqrt(rate)
    n = jnp.arange(TERMS, dtype=jnp.float32)
    fact = jnp.cumprod(jnp.maximum(n, 1.0))
    powers = (-8.0 * rate)[None] ** n[:, None, None] / fact[:, None, None]
    l75 = jnp.exp(-7.5 * rate)
    cs = l75[None] * powers
    ci = jnp.sum(weight[None] * cs, axis=1)
    inter = ((weight * jnp.exp(-8.5 * rate))[None] * powers).transpose(1, 0, 2)
    l16 = jnp.exp(-float(SUB) * rate)
    phi, mom, psi = bases(rows)
    grid = (chans // lanes, blocks)
    subs_terms = mom.shape[0]
    params = pltpu.CompilerParams(dimension_semantics=("arbitrary", "arbitrary"))

    wide = min(STATE_BLOCK, count)
    _, mom_wide, _ = bases(wide)
    final = pl.pallas_call(
        state_kernel,
        grid=(chans // lanes, count // wide),
        in_specs=[
            pl.BlockSpec((wide, lanes), lambda j, b: (b, j)),
            pl.BlockSpec(mom_wide.shape, lambda j, b: (0, 0)),
            pl.BlockSpec((TERMS, modes, lanes), lambda j, b: (0, 0, j)),
            pl.BlockSpec((modes, lanes), lambda j, b: (0, j)),
        ],
        out_specs=pl.BlockSpec((modes, lanes), lambda j, b: (0, j)),
        out_shape=jax.ShapeDtypeStruct((modes, chans), jnp.float32),
        scratch_shapes=[pltpu.VMEM((modes, lanes), jnp.float32)],
        compiler_params=params,
    )(lr_input, mom_wide, cs, l16)

    devices = lax.axis_size("ctx")
    incoming = jnp.zeros_like(final)
    for shift in range(1, devices):
        earlier = passed_along(final, "ctx", shift)
        incoming = incoming + jnp.exp(-rate * float((shift - 1) * count)) * earlier

    return pl.pallas_call(
        main_kernel,
        grid=grid,
        in_specs=[
            pl.BlockSpec((rows, lanes), lambda j, b: (b, j)),
            pl.BlockSpec((rows, lanes), lambda j, b: (b, j)),
            pl.BlockSpec((TERMS * rows, 2 * rows), lambda j, b: (0, 0)),
            pl.BlockSpec((subs_terms, 2 * rows), lambda j, b: (0, 0)),
            pl.BlockSpec((rows, 3 * subs_terms), lambda j, b: (0, 0)),
            pl.BlockSpec((TERMS, lanes), lambda j, b: (0, j)),
            pl.BlockSpec((TERMS, modes, lanes), lambda j, b: (0, 0, j)),
            pl.BlockSpec((modes, TERMS, lanes), lambda j, b: (0, 0, j)),
            pl.BlockSpec((modes, lanes), lambda j, b: (0, j)),
            pl.BlockSpec((modes, lanes), lambda j, b: (0, j)),
            pl.BlockSpec((1, lanes), lambda j, b: (0, j)),
        ],
        out_specs=pl.BlockSpec((rows, lanes), lambda j, b: (b, j)),
        out_shape=jax.ShapeDtypeStruct((count, chans), jnp.bfloat16),
        scratch_shapes=[pltpu.VMEM((modes, lanes), jnp.float32)],
        compiler_params=params,
    )(lr_input, gate0, phi, mom, psi, ci, cs, inter, l16, incoming, lr_skip[None, :])


HALO = 144


def front_kernel(feat_ref, halo_ref, sf_ref, rows_ref, gate_ref, o_ref, ext_ref, prod_ref):
    count = feat_ref.shape[1]
    lanes = feat_ref.shape[2]
    groups = rows_ref.shape[0]
    taps = rows_ref.shape[1] // 2
    width = sf_ref.shape[1]
    toep = [
        pltpu.roll(
            jnp.broadcast_to(rows_ref[g : g + 1, :], (taps, 2 * taps)), 0, 1, stride=1, stride_axis=0
        ).astype(jnp.bfloat16)
        for g in range(groups)
    ]
    for i in range(3):
        ext_ref[i, 0:HALO, :] = halo_ref[i].astype(jnp.float32)
        ext_ref[i, HALO : HALO + count, :] = feat_ref[i].astype(jnp.float32)
    taps_row = [[sf_ref[i, j : j + 1, :] for j in range(width)] for i in range(3)]

    def plane(i, e0):
        total = taps_row[i][0] * ext_ref[i, e0 : e0 + taps, :]
        for j in range(1, width):
            total = total + taps_row[i][j] * ext_ref[i, e0 - j : e0 - j + taps, :]
        return total

    lane_group = lax.broadcasted_iota(jnp.int32, (taps, lanes), 1) // (lanes // groups)
    for t0 in range(-taps, count, taps):
        e0 = t0 + HALO
        prod = (plane(1, e0) * plane(2, e0)).astype(jnp.bfloat16)
        prod_ref[e0 : e0 + taps, :] = prod
        if t0 < 0:
            continue
        window = prod_ref[e0 - taps : e0 + taps, :]
        mixed = None
        for g in range(groups):
            res = jnp.dot(toep[g], window, preferred_element_type=jnp.float32)
            mixed = res if mixed is None else jnp.where(lane_group == g, res, mixed)
        query = plane(0, e0)
        gate = gate_ref[t0 : t0 + taps, :].astype(jnp.float32)
        o_ref[t0 : t0 + taps, :] = (gate * query * mixed).astype(o_ref.dtype)


def front(planes, halo, short_filter, mr_filter, gate1):
    _, count, chans = planes.shape
    groups, taps = mr_filter.shape
    lanes = 128
    per_tile = lanes // (chans // groups)
    template = jnp.concatenate(
        [
            jnp.zeros((groups, 1), jnp.float32),
            mr_filter[:, ::-1].astype(jnp.float32),
            jnp.zeros((groups, taps - 1), jnp.float32),
        ],
        1,
    )
    sf = short_filter.transpose(1, 0, 2)
    width = sf.shape[1]
    return pl.pallas_call(
        front_kernel,
        grid=(chans // lanes,),
        in_specs=[
            pl.BlockSpec((3, count, lanes), lambda j: (0, 0, j)),
            pl.BlockSpec((3, HALO, lanes), lambda j: (0, 0, j)),
            pl.BlockSpec((3, width, lanes), lambda j: (0, 0, j)),
            pl.BlockSpec((per_tile, 2 * taps), lambda j: (j, 0)),
            pl.BlockSpec((count, lanes), lambda j: (0, j)),
        ],
        out_specs=pl.BlockSpec((count, lanes), lambda j: (0, j)),
        out_shape=jax.ShapeDtypeStruct((count, chans), jnp.bfloat16),
        scratch_shapes=[
            pltpu.VMEM((3, HALO + count, lanes), jnp.float32),
            pltpu.VMEM((HALO + count, lanes), jnp.bfloat16),
        ],
        compiler_params=pltpu.CompilerParams(dimension_semantics=("arbitrary",)),
    )(planes, halo, sf, template, gate1)


def per_device(features, short_filter, mr_filter, lr_gates, lr_rate, lr_residue, lr_skip):
    count = features.shape[0]
    planes = features.transpose(1, 0, 2)
    halo = passed_along(planes[:, count - HALO :], "ctx", 1)
    gates = lr_gates.transpose(1, 0, 2)
    lr_input = front(planes, halo, short_filter, mr_filter, gates[1])
    return long_conv_out(lr_input, gates[0], lr_rate, lr_residue, lr_skip)


def solution(mesh):
    in_specs = (
        P(("groups", "ctx"), None, ("mp", "sub")),
        P(None, None, ("mp", "sub")),
        P(("mp", "sub"), None),
        P(("groups", "ctx"), None, ("mp", "sub")),
        P(("mp", "sub"), None),
        P(("mp", "sub"), None),
        P(("mp", "sub")),
    )
    out_specs = P(("groups", "ctx"), ("mp", "sub"))
    return jax.shard_map(
        per_device, mesh=mesh, in_specs=in_specs, out_specs=out_specs, check_vma=False
    )
```

```python
import functools

import jax
import numpy as np
import jax.numpy as jnp
from jax import lax
from jax.experimental import pallas as pl
from jax.experimental.pallas import tpu as pltpu
from jax.sharding import PartitionSpec as P

TAPS = 128
SHORT = 7
BLOCK = 128
STATE_BLOCK = 256
LANES = 1024


def passed_along(shard, axis, by):
    devices = lax.axis_size(axis)
    pairs = [(i, i + by) for i in range(devices) if 0 <= i + by < devices]
    return lax.ppermute(shard, axis, pairs)


def featurize(extended, weights):
    width = weights.shape[0]
    count = extended.shape[0] - (width - 1)
    total = jnp.zeros((count,) + extended.shape[1:], jnp.float32)
    for j in range(width):
        total = total + weights[j] * extended[width - 1 - j : width - 1 - j + count]
    return total


def medium_mix(extended, filters):
    groups, taps = filters.shape
    rows = extended.shape[0] - (taps - 1)
    chans = extended.shape[1]
    padded = jnp.concatenate([jnp.zeros((1, chans), jnp.bfloat16), extended], 0)
    blocks = rows // taps
    before = padded[:rows].reshape(blocks, taps, chans)
    current = padded[taps:].reshape(blocks, taps, chans)
    window = jnp.concatenate([before, current], 1).reshape(
        blocks, 2 * taps, groups, chans // groups
    )
    window = window.transpose(2, 3, 0, 1)
    lag = jnp.arange(taps)[:, None] + taps - jnp.arange(2 * taps)[None, :]
    pick = (lag[None] == jnp.arange(taps)[:, None, None]).astype(jnp.bfloat16)
    toeplitz = jnp.einsum("gj,jts->gts", filters, pick, preferred_element_type=jnp.float32)
    toeplitz = toeplitz.astype(jnp.bfloat16)
    mixed = jnp.einsum("gts,gkbs->gkbt", toeplitz, window, preferred_element_type=jnp.float32)
    return mixed.transpose(2, 3, 0, 1).reshape(rows, chans)


SUB = 16
TERMS = 8


def split_pair(values):
    high = values.astype(jnp.bfloat16)
    low = (values - high.astype(jnp.float32)).astype(jnp.bfloat16)
    return high, low


def tree_sum(values):
    while len(values) > 1:
        values = [values[i] + values[i + 1] if i + 1 < len(values) else values[i] for i in range(0, len(values), 2)]
    return values[0]


def carry_subblocks(moments, z, cs_ref, l16, inter_ref=None):
    terms = cs_ref.shape[0]
    subs = moments.shape[0] // terms
    coefs = [cs_ref[n] for n in range(terms)]
    accs = [
        tree_sum([coefs[n] * moments[sb * terms + n : sb * terms + n + 1] for n in range(terms)])
        for sb in range(subs)
    ]
    zs = []
    for sb in range(subs):
        zs.append(z)
        z = l16 * z + accs[sb]
    parts = []
    if inter_ref is not None:
        modes = z.shape[0]
        for sb in range(subs):
            parts.append(tree_sum([inter_ref[r] * zs[sb][r : r + 1] for r in range(modes)]))
    return z, parts


def state_kernel(x_ref, mom_ref, cs_ref, l16_ref, f_ref, z_ref):
    b = pl.program_id(1)

    @pl.when(b == 0)
    def _():
        z_ref[...] = jnp.zeros_like(z_ref)

    xb = x_ref[...]
    moments = jnp.dot(mom_ref[...], jnp.concatenate([xb, xb], 0), preferred_element_type=jnp.float32)
    z, _ = carry_subblocks(moments, z_ref[...], cs_ref, l16_ref[...])
    z_ref[...] = z

    @pl.when(b == pl.num_programs(1) - 1)
    def _():
        f_ref[...] = z


def main_kernel(x_ref, gate_ref, phi_ref, mom_ref, psi_ref, ci_ref, cs_ref, inter_ref, l16_ref,
                zin_ref, skip_ref, o_ref, z_ref):
    b = pl.program_id(1)

    @pl.when(b == 0)
    def _():
        z_ref[...] = zin_ref[...]

    xb = x_ref[...]
    rows = xb.shape[0]
    x2 = jnp.concatenate([xb, xb], 0)
    near = jnp.dot(phi_ref[...], x2, preferred_element_type=jnp.float32)
    y = tree_sum([ci_ref[n : n + 1] * near[n * rows : (n + 1) * rows] for n in range(ci_ref.shape[0])])
    moments = jnp.dot(mom_ref[...], x2, preferred_element_type=jnp.float32)
    z, parts = carry_subblocks(moments, z_ref[...], cs_ref, l16_ref[...], inter_ref)
    z_ref[...] = z
    high, low = split_pair(jnp.concatenate(parts, 0))
    far = jnp.dot(psi_ref[...], jnp.concatenate([high, low, high], 0), preferred_element_type=jnp.float32)
    total = y + far + skip_ref[...] * xb.astype(jnp.float32)
    o_ref[...] = (gate_ref[...].astype(jnp.float32) * total).astype(o_ref.dtype)


def np_split(values):
    high = values.astype(jnp.bfloat16)
    low = (values - high.astype(np.float64)).astype(jnp.bfloat16)
    return high, low


def bases(rows):
    subs = rows // SUB
    n = np.arange(TERMS, dtype=np.float64)
    t = np.arange(rows)
    sb, tl = t // SUB, (t % SUB).astype(np.float64)
    same = sb[:, None] == sb[None, :]
    lag = (t[:, None] - t[None, :]).astype(np.float64)
    near = np.where(
        (same & (lag >= 0))[None], ((lag - 7.5) / 8.0)[None] ** n[:, None, None], 0.0
    ).reshape(TERMS * rows, rows)
    own = np.arange(subs)[:, None] == sb[None, :]
    mom = np.where(own[:, None, :], ((7.5 - tl) / 8.0)[None, None, :] ** n[None, :, None], 0.0)
    mom = mom.reshape(subs * TERMS, rows)
    psi = np.where(own.T[:, :, None], ((tl - 7.5) / 8.0)[:, None, None] ** n[None, None, :], 0.0)
    psi = psi.reshape(rows, subs * TERMS)
    nh, nl = np_split(near)
    mh, ml = np_split(mom)
    ph, pl_ = np_split(psi)
    return (
        jnp.asarray(np.concatenate([nh, nl], 1)),
        jnp.asarray(np.concatenate([mh, ml], 1)),
        jnp.asarray(np.concatenate([ph, ph, pl_], 1)),
    )


def long_conv_out(lr_input, gate0, lr_rate, lr_residue, lr_skip):
    count, chans = lr_input.shape
    modes = lr_rate.shape[1]
    rows = BLOCK
    lanes = min(LANES, chans)
    blocks = count // rows
    rate = lr_rate.T
    weight = lr_residue.T * jnp.sqrt(rate)
    n = jnp.arange(TERMS, dtype=jnp.float32)
    fact = jnp.cumprod(jnp.maximum(n, 1.0))
    powers = (-8.0 * rate)[None] ** n[:, None, None] / fact[:, None, None]
    l75 = jnp.exp(-7.5 * rate)
    cs = l75[None] * powers
    ci = jnp.sum(weight[None] * cs, axis=1)
    inter = ((weight * jnp.exp(-8.5 * rate))[None] * powers).transpose(1, 0, 2)
    l16 = jnp.exp(-float(SUB) * rate)
    phi, mom, psi = bases(rows)
    grid = (chans // lanes, blocks)
    subs_terms = mom.shape[0]
    params = pltpu.CompilerParams(dimension_semantics=("arbitrary", "arbitrary"))

    wide = min(STATE_BLOCK, count)
    _, mom_wide, _ = bases(wide)
    final = pl.pallas_call(
        state_kernel,
        grid=(chans // lanes, count // wide),
        in_specs=[
            pl.BlockSpec((wide, lanes), lambda j, b: (b, j)),
            pl.BlockSpec(mom_wide.shape, lambda j, b: (0, 0)),
            pl.BlockSpec((TERMS, modes, lanes), lambda j, b: (0, 0, j)),
            pl.BlockSpec((modes, lanes), lambda j, b: (0, j)),
        ],
        out_specs=pl.BlockSpec((modes, lanes), lambda j, b: (0, j)),
        out_shape=jax.ShapeDtypeStruct((modes, chans), jnp.float32),
        scratch_shapes=[pltpu.VMEM((modes, lanes), jnp.float32)],
        compiler_params=params,
    )(lr_input, mom_wide, cs, l16)

    devices = lax.axis_size("ctx")
    incoming = jnp.zeros_like(final)
    for shift in range(1, devices):
        earlier = passed_along(final, "ctx", shift)
        incoming = incoming + jnp.exp(-rate * float((shift - 1) * count)) * earlier

    return pl.pallas_call(
        main_kernel,
        grid=grid,
        in_specs=[
            pl.BlockSpec((rows, lanes), lambda j, b: (b, j)),
            pl.BlockSpec((rows, lanes), lambda j, b: (b, j)),
            pl.BlockSpec((TERMS * rows, 2 * rows), lambda j, b: (0, 0)),
            pl.BlockSpec((subs_terms, 2 * rows), lambda j, b: (0, 0)),
            pl.BlockSpec((rows, 3 * subs_terms), lambda j, b: (0, 0)),
            pl.BlockSpec((TERMS, lanes), lambda j, b: (0, j)),
            pl.BlockSpec((TERMS, modes, lanes), lambda j, b: (0, 0, j)),
            pl.BlockSpec((modes, TERMS, lanes), lambda j, b: (0, 0, j)),
            pl.BlockSpec((modes, lanes), lambda j, b: (0, j)),
            pl.BlockSpec((modes, lanes), lambda j, b: (0, j)),
            pl.BlockSpec((1, lanes), lambda j, b: (0, j)),
        ],
        out_specs=pl.BlockSpec((rows, lanes), lambda j, b: (b, j)),
        out_shape=jax.ShapeDtypeStruct((count, chans), jnp.bfloat16),
        scratch_shapes=[pltpu.VMEM((modes, lanes), jnp.float32)],
        compiler_params=params,
    )(lr_input, gate0, phi, mom, psi, ci, cs, inter, l16, incoming, lr_skip[None, :])


HALO = 144


def front_kernel(feat_ref, halo_ref, sf_ref, rows_ref, gate_ref, o_ref, ext_ref, prod_ref):
    count = feat_ref.shape[1]
    lanes = feat_ref.shape[2]
    groups = rows_ref.shape[0]
    taps = rows_ref.shape[1] // 2
    width = sf_ref.shape[1]
    toep = [
        pltpu.roll(
            jnp.broadcast_to(rows_ref[g : g + 1, :], (taps, 2 * taps)), 0, 1, stride=1, stride_axis=0
        ).astype(jnp.bfloat16)
        for g in range(groups)
    ]
    for i in range(3):
        ext_ref[i, 0:HALO, :] = halo_ref[i].astype(jnp.float32)
        ext_ref[i, HALO : HALO + count, :] = feat_ref[i].astype(jnp.float32)
    taps_row = [[sf_ref[i, j : j + 1, :] for j in range(width)] for i in range(3)]

    def plane(i, e0):
        total = taps_row[i][0] * ext_ref[i, e0 : e0 + taps, :]
        for j in range(1, width):
            total = total + taps_row[i][j] * ext_ref[i, e0 - j : e0 - j + taps, :]
        return total

    lane_group = lax.broadcasted_iota(jnp.int32, (taps, lanes), 1) // (lanes // groups)
    for t0 in range(-taps, count, taps):
        e0 = t0 + HALO
        prod = (plane(1, e0) * plane(2, e0)).astype(jnp.bfloat16)
        prod_ref[e0 : e0 + taps, :] = prod
        if t0 < 0:
            continue
        window = prod_ref[e0 - taps : e0 + taps, :]
        mixed = None
        for g in range(groups):
            res = jnp.dot(toep[g], window, preferred_element_type=jnp.float32)
            mixed = res if mixed is None else jnp.where(lane_group == g, res, mixed)
        query = plane(0, e0)
        gate = gate_ref[t0 : t0 + taps, :].astype(jnp.float32)
        o_ref[t0 : t0 + taps, :] = (gate * query * mixed).astype(o_ref.dtype)


def front(planes, halo, short_filter, mr_filter, gate1):
    _, count, chans = planes.shape
    groups, taps = mr_filter.shape
    lanes = 128
    per_tile = lanes // (chans // groups)
    template = jnp.concatenate(
        [
            jnp.zeros((groups, 1), jnp.float32),
            mr_filter[:, ::-1].astype(jnp.float32),
            jnp.zeros((groups, taps - 1), jnp.float32),
        ],
        1,
    )
    sf = short_filter.transpose(1, 0, 2)
    width = sf.shape[1]
    return pl.pallas_call(
        front_kernel,
        grid=(chans // lanes,),
        in_specs=[
            pl.BlockSpec((3, count, lanes), lambda j: (0, 0, j)),
            pl.BlockSpec((3, HALO, lanes), lambda j: (0, 0, j)),
            pl.BlockSpec((3, width, lanes), lambda j: (0, 0, j)),
            pl.BlockSpec((per_tile, 2 * taps), lambda j: (j, 0)),
            pl.BlockSpec((count, lanes), lambda j: (0, j)),
        ],
        out_specs=pl.BlockSpec((count, lanes), lambda j: (0, j)),
        out_shape=jax.ShapeDtypeStruct((count, chans), jnp.bfloat16),
        scratch_shapes=[
            pltpu.VMEM((3, HALO + count, lanes), jnp.float32),
            pltpu.VMEM((HALO + count, lanes), jnp.bfloat16),
        ],
        compiler_params=pltpu.CompilerParams(dimension_semantics=("arbitrary",)),
    )(planes, halo, sf, template, gate1)


def per_device(features, short_filter, mr_filter, lr_gates, lr_rate, lr_residue, lr_skip):
    count = features.shape[0]
    planes = features.transpose(1, 0, 2)
    halo = passed_along(planes[:, count - HALO :], "ctx", 1)
    gates = lr_gates.transpose(1, 0, 2)
    lr_input = front(planes, halo, short_filter, mr_filter, gates[1])
    return long_conv_out(lr_input, gates[0], lr_rate, lr_residue, lr_skip)


def solution(mesh):
    in_specs = (
        P(("groups", "ctx"), None, ("mp", "sub")),
        P(None, None, ("mp", "sub")),
        P(("mp", "sub"), None),
        P(("groups", "ctx"), None, ("mp", "sub")),
        P(("mp", "sub"), None),
        P(("mp", "sub"), None),
        P(("mp", "sub")),
    )
    out_specs = P(("groups", "ctx"), ("mp", "sub"))
    return jax.shard_map(
        per_device, mesh=mesh, in_specs=in_specs, out_specs=out_specs, check_vma=False
    )
```
